256 devices in a mesh: obs: 4 (over y), blk: 64 (over x, z, core).
Axes of the slice: x: 4, y: 4, z: 8, core: 2. Of those that a mesh axis runs over, the one named last changes fastest.
Arguments:
- design_tiles: float32 [32768, 8, 128], P(('obs', 'blk')), may hold values from -8 to 8
- block_ids: int32 [32768, 8], P(('obs', 'blk')), may hold values from 0 to 63, as said below
- obs_weight: float32 [32768], P(('obs', 'blk')), may hold values from 4.8828126e-05 to 0.00048828125
- block_owner: int32 [64], replicated, may hold values from 0 to 63, each once
- prior_weight: float32 [512], replicated, may hold values from 0.25 to 1
Outputs:
- panel_factor: float32 [8192, 256], P('blk')
- panel_update: float32 [8192, 256], P('blk')
The draws below stay inside these ranges and needn't reach their ends.
Inputs may be any that keep to these rules, and one draw needn't show every extreme that they name: `block_ids`: the 8 blocks of an observation are distinct. Among the 128 observations of one device (aligned blocks of rows) no block is named by more than 24 of them, and in every draw some device has a block named by exactly 24. `block_owner`: A permutation: each owner index once.
All inputs are finite; a program needn't handle non-finite values.
Results may differ from the reference program's by a relative error of at most 0.0003.
Values sent between devices are 32-bit elements; how exact they have to be, the bound alone decides.
No kernel may reach another device: no remote copies, remote signals or barrier semaphores. Data moves between devices by JAX's collectives and lax.ppermute only.
A program may use at most 64 MiB of HBM per device.

```python
import math
import jax
import jax.numpy as jnp
from jax import lax

BLOCK = 128
PW = 256
K = 8
OBS_DEV = 128
NBLK = 64
CAP = 24
OBS_ALL = 32768


def draw_design_tiles(key, part):
    key_common = jax.random.fold_in(key, 11)
    key_single = jax.random.fold_in(key, 12)
    common = jax.random.normal(key_common, (OBS_ALL, 1, BLOCK), jnp.float32)
    single = jax.random.normal(key_single, (OBS_ALL, K, BLOCK), jnp.float32)
    values = common + single
    return jnp.clip(values, -8.0, 8.0)


def draw_block_ids(key, part):
    slot_total = OBS_DEV * K
    rest_count = NBLK - 1
    rest_base = (slot_total - CAP) // rest_count
    rest_extra = slot_total - CAP - rest_base * rest_count
    spread_most = max(0, min(CAP - rest_base - 1, rest_base - 1))
    device_count = OBS_ALL // OBS_DEV

    def device_table(device_key):
        key_skew = jax.random.fold_in(device_key, 21)
        key_perm = jax.random.fold_in(device_key, 22)
        key_rows = jax.random.fold_in(device_key, 23)
        block_label = jnp.arange(NBLK, dtype=jnp.int32)
        spread = jax.random.randint(key_skew, (NBLK,), 0, spread_most + 1, dtype=jnp.int32)
        shifted = block_label - 1
        pair_index = jnp.maximum(shifted, 0) // 2
        paired = (block_label >= 1) & (shifted < 2 * (rest_count // 2))
        pair_sign = 1 - 2 * (jnp.maximum(shifted, 0) % 2)
        counts = rest_base + (shifted < rest_extra).astype(jnp.int32)
        counts = counts + jnp.where(paired, pair_sign * spread[pair_index], 0)
        counts = jnp.where(block_label == 0, CAP, counts).astype(jnp.int32)
        bounds = jnp.cumsum(counts).astype(jnp.int32)
        position = jnp.arange(slot_total, dtype=jnp.int32)
        sorted_labels = jnp.sum((position[:, None] >= bounds[None, :]).astype(jnp.int32), axis=1)
        relabel = jax.random.permutation(key_perm, NBLK).astype(jnp.int32)
        id_table = relabel[sorted_labels].reshape(K, OBS_DEV).T
        row_order = jax.random.permutation(key_rows, OBS_DEV).astype(jnp.int32)
        return id_table[row_order].astype(jnp.int32)
    device_keys = jax.random.split(jax.random.fold_in(key, 31), device_count)
    tables = lax.map(device_table, device_keys)
    return tables.reshape(OBS_ALL, K).astype(jnp.int32)


def levels(rng, shape, pieces, smallest, top_value):
    factor_of = 1.0
    for dim, parts in pieces:
        heights = jax.random.uniform(jax.random.fold_in(jax.random.fold_in(rng, 6), dim), (parts,), jnp.float32, smallest / len(pieces), top_value / len(pieces))
        factor_of = factor_of * jnp.repeat(jnp.exp(heights), shape[dim] // parts).reshape((-1,) + (1,) * (len(shape) - 1 - dim))
    return factor_of


def setup_inputs(seed: int = 0) -> dict:
    keys = jax.random.split(jax.random.key(seed), 6)
    return {
        "design_tiles": draw_design_tiles(jax.random.fold_in(keys[5], 71), 0),
        "block_ids": draw_block_ids(jax.random.fold_in(keys[5], 71), 0),
        "obs_weight": jnp.clip(jnp.exp(math.log(0.00048828125) - 2.3025851 * jax.random.uniform(keys[2], (OBS_ALL,), jnp.float32) ** levels(keys[2], (OBS_ALL,), ((0, 256),), -0.2, 0.2)), 4.882812572759576e-05, 0.00048828125),
        "block_owner": jax.random.permutation(keys[3], NBLK).astype(jnp.int32),
        "prior_weight": jnp.clip(jnp.exp(jax.random.uniform(keys[4], (2 * PW,), jnp.float32, math.log(0.25), math.log(1.0))), 0.25, 1.0),
    }


def back_solve(factor, right_rows):
    return jax.scipy.linalg.solve_triangular(factor, right_rows.T, lower=True).T

def reference(design_tiles, block_ids, obs_weight, block_owner, prior_weight):
    total_rows = NBLK * BLOCK
    panel_cols = 2 * PW
    batch_rows = min(OBS_ALL, 512)
    batches = OBS_ALL // batch_rows
    block_range = jnp.arange(NBLK, dtype=jnp.int32)

    def accumulate(total, batch_index):
        start = batch_index * batch_rows
        tiles_now = lax.dynamic_slice_in_dim(design_tiles, start, batch_rows, 0)
        ids_now = lax.dynamic_slice_in_dim(block_ids, start, batch_rows, 0)
        weight_now = lax.dynamic_slice_in_dim(obs_weight, start, batch_rows, 0)
        one_hot = (ids_now[:, :, None] == block_range[None, None, :]).astype(jnp.float32)
        design = jnp.einsum('okb,okj->obj', one_hot, tiles_now, precision=lax.Precision.HIGHEST)
        design = design.reshape(batch_rows, total_rows)
        weighted = design[:, :panel_cols] * weight_now[:, None]
        total = total + jnp.einsum('oi,op->ip', design, weighted, precision=lax.Precision.HIGHEST)
        return (total, None)
    normal, _ = lax.scan(accumulate, jnp.zeros((total_rows, panel_cols), jnp.float32), jnp.arange(batches, dtype=jnp.int32))
    diag_index = jnp.arange(panel_cols, dtype=jnp.int32)
    normal = normal.at[diag_index, diag_index].add(prior_weight)
    square = normal[:panel_cols]
    mirrored = 0.5 * (square + square.T)
    factor = jnp.linalg.cholesky(mirrored[:PW, :PW])
    coupling = back_solve(factor, mirrored[PW:, :PW])
    first_rows = back_solve(factor, normal[:, :PW])
    update_rows = normal[:, PW:] - jnp.dot(first_rows.astype(jnp.float32), coupling.T.astype(jnp.float32), precision=lax.Precision.HIGHEST, preferred_element_type=jnp.float32)
    slot_order = jnp.zeros((NBLK,), jnp.int32).at[block_owner].set(block_range)
    panel_factor = first_rows.reshape(NBLK, BLOCK, PW)[slot_order].reshape(total_rows, PW)
    panel_update = update_rows.reshape(NBLK, BLOCK, PW)[slot_order].reshape(total_rows, PW)
    return (panel_factor, panel_update)
```

```python
import jax
import jax.numpy as jnp
from jax import lax
from jax.sharding import PartitionSpec as P

CAP = 24
HI = lax.Precision.HIGHEST


def back_solve(factor, right_rows):
    return jax.scipy.linalg.solve_triangular(factor, right_rows.T, lower=True).T


def select_columns(labels, design_tiles, wanted):
    touched = design_tiles.shape[1]
    columns = jnp.zeros(
        (design_tiles.shape[0], wanted.shape[0], design_tiles.shape[2]), jnp.float32
    )
    for entry in range(touched):
        hit = labels[:, entry, None] == wanted[None, :]
        columns = columns + jnp.where(hit[:, :, None], design_tiles[:, entry, None, :], 0.0)
    return columns.reshape(design_tiles.shape[0], wanted.shape[0] * design_tiles.shape[2])


def obs_butterfly(x):
    n = lax.axis_size("obs")
    step = 1
    while step < n:
        perm = [(i, i ^ step) for i in range(n)]
        x = x + lax.ppermute(x, "obs", perm)
        step *= 2
    return x


def local(design_tiles, block_ids, obs_weight, block_owner, prior_weight):
    n_obs, touched, bw = design_tiles.shape
    nblk = block_owner.shape[0]
    panel_cols = prior_weight.shape[0]
    half = panel_cols // 2
    panel_blocks = panel_cols // bw
    nb = lax.axis_size("blk")
    my_j = lax.axis_index("blk")
    block_range = jnp.arange(nblk, dtype=jnp.int32)
    dest_range = jnp.arange(nb, dtype=jnp.int32)

    inv_owner = jnp.sum(
        jnp.where(block_owner[None, :] == dest_range[:, None], block_range[None, :], 0), axis=1
    )
    slot_owner = jnp.sum(
        jnp.where(block_ids[:, :, None] == block_range[None, None, :], block_owner[None, None, :], 0),
        axis=2,
    )
    hit = slot_owner[:, :, None] == dest_range[None, None, :]
    touch = jnp.sum(hit.astype(jnp.int32), axis=1)
    cum = jnp.cumsum(touch, axis=0)
    rank_range = jnp.arange(CAP, dtype=jnp.int32)
    obs_sel = jnp.sum((cum[:, :, None] <= rank_range[None, None, :]).astype(jnp.int32), axis=0)
    valid = rank_range[None, :] < cum[-1][:, None]
    obs_sel = jnp.minimum(obs_sel, n_obs - 1)
    owners_sel = slot_owner[obs_sel]
    k_sel = jnp.sum(
        jnp.where(owners_sel == dest_range[:, None, None], jnp.arange(touched, dtype=jnp.int32), 0),
        axis=2,
    )
    flat_tiles = design_tiles.reshape(n_obs * touched, bw)
    tile_rows = flat_tiles[obs_sel * touched + k_sel]

    panel_design = select_columns(
        block_ids, design_tiles, jnp.arange(panel_blocks, dtype=jnp.int32)
    )
    weighted = panel_design * obs_weight[:, None]
    panel_rows = weighted[obs_sel]
    tile_rows = jnp.where(valid[:, :, None], tile_rows, 0.0)
    panel_rows = jnp.where(valid[:, :, None], panel_rows, 0.0)

    gram = jnp.einsum("op,oq->pq", weighted, panel_design[:, :half], precision=HI)
    gram_rows = panel_cols // nb
    payload = jnp.concatenate(
        [
            tile_rows.reshape(nb, CAP * bw),
            panel_rows.reshape(nb, CAP * panel_cols),
            gram.reshape(nb, gram_rows * half),
        ],
        axis=1,
    )
    got = lax.all_to_all(payload, "blk", 0, 0, tiled=True)
    got_tiles = got[:, : CAP * bw].reshape(nb * CAP, bw)
    got_panel = got[:, CAP * bw : CAP * (bw + panel_cols)].reshape(nb * CAP, panel_cols)
    got_gram = got[:, CAP * (bw + panel_cols) :].reshape(nb, gram_rows * half)
    owned = jnp.einsum("si,sp->ip", got_tiles, got_panel, precision=HI)
    gram_part = jnp.sum(got_gram, axis=0)

    both = obs_butterfly(jnp.concatenate([owned.reshape(-1), gram_part]))
    owned = both[: bw * panel_cols].reshape(bw, panel_cols)
    gram_part = both[bw * panel_cols :]

    spread = jnp.broadcast_to(gram_part[None, :], (nb, gram_rows * half))
    square = lax.all_to_all(spread, "blk", 0, 0, tiled=True).reshape(panel_cols, half)
    diag = jnp.arange(half, dtype=jnp.int32)
    square = square.at[diag, diag].add(prior_weight[:half])

    my_block = jnp.sum(jnp.where(block_owner == my_j, block_range, 0))
    row_index = my_block * bw + jnp.arange(bw, dtype=jnp.int32)
    col_index = jnp.arange(panel_cols, dtype=jnp.int32)
    owned = owned + jnp.where(col_index[None, :] == row_index[:, None], prior_weight[None, :], 0.0)

    top = square[:half]
    mirrored = 0.5 * (top + top.T)
    factor = jnp.linalg.cholesky(mirrored)
    coupling = back_solve(factor, square[half:])
    first_rows = back_solve(factor, owned[:, :half])
    update_rows = owned[:, half:] - jnp.dot(
        first_rows, coupling.T, precision=HI, preferred_element_type=jnp.float32
    )
    return (first_rows, update_rows)


def solution(mesh):
    in_specs = (P(("obs", "blk"), None, None), P(("obs", "blk"), None), P(("obs", "blk")), P(), P())
    out_specs = (P("blk", None), P("blk", None))
    return jax.shard_map(local, mesh=mesh, in_specs=in_specs, out_specs=out_specs, check_vma=False)
```

```python
import jax
import jax.numpy as jnp
from jax import lax
from jax.sharding import PartitionSpec as P

CAP = 24
HI = lax.Precision.HIGHEST
SPLIT = 2


def pl_slice(chunk, size):
    return slice(chunk * size, (chunk + 1) * size)


def back_solve(factor, right_rows):
    return jax.scipy.linalg.solve_triangular(factor, right_rows.T, lower=True).T


def select_columns(labels, design_tiles, wanted):
    touched = design_tiles.shape[1]
    columns = jnp.zeros(
        (design_tiles.shape[0], wanted.shape[0], design_tiles.shape[2]), jnp.float32
    )
    for entry in range(touched):
        hit = labels[:, entry, None] == wanted[None, :]
        columns = columns + jnp.where(hit[:, :, None], design_tiles[:, entry, None, :], 0.0)
    return columns.reshape(design_tiles.shape[0], wanted.shape[0] * design_tiles.shape[2])


def obs_butterfly(x):
    n = lax.axis_size("obs")
    step = 1
    while step < n:
        perm = [(i, i ^ step) for i in range(n)]
        x = x + lax.ppermute(x, "obs", perm)
        step *= 2
    return x


def local(design_tiles, block_ids, obs_weight, block_owner, prior_weight):
    n_obs, touched, bw = design_tiles.shape
    nblk = block_owner.shape[0]
    panel_cols = prior_weight.shape[0]
    half = panel_cols // 2
    panel_blocks = panel_cols // bw
    nb = lax.axis_size("blk")
    my_j = lax.axis_index("blk")
    block_range = jnp.arange(nblk, dtype=jnp.int32)
    dest_range = jnp.arange(nb, dtype=jnp.int32)

    inv_owner = jnp.sum(
        jnp.where(block_owner[None, :] == dest_range[:, None], block_range[None, :], 0), axis=1
    )
    slot_owner = jnp.sum(
        jnp.where(block_ids[:, :, None] == block_range[None, None, :], block_owner[None, None, :], 0),
        axis=2,
    )
    hit = slot_owner[:, :, None] == dest_range[None, None, :]
    touch = jnp.sum(hit.astype(jnp.int32), axis=1)
    cum = jnp.cumsum(touch, axis=0)
    rank_range = jnp.arange(CAP, dtype=jnp.int32)
    obs_sel = jnp.sum((cum[:, :, None] <= rank_range[None, None, :]).astype(jnp.int32), axis=0)
    valid = rank_range[None, :] < cum[-1][:, None]
    obs_sel = jnp.minimum(obs_sel, n_obs - 1)
    owners_sel = slot_owner[obs_sel]
    k_sel = jnp.sum(
        jnp.where(owners_sel == dest_range[:, None, None], jnp.arange(touched, dtype=jnp.int32), 0),
        axis=2,
    )
    flat_tiles = design_tiles.reshape(n_obs * touched, bw)
    tile_rows = flat_tiles[obs_sel * touched + k_sel]

    panel_design = select_columns(
        block_ids, design_tiles, jnp.arange(panel_blocks, dtype=jnp.int32)
    )
    weighted = panel_design * obs_weight[:, None]
    panel_rows = weighted[obs_sel]
    tile_rows = jnp.where(valid[:, :, None], tile_rows, 0.0)
    panel_rows = jnp.where(valid[:, :, None], panel_rows, 0.0)

    gram = jnp.einsum("op,oq->pq", weighted, panel_design[:, :half], precision=HI)
    gram_rows = panel_cols // nb
    got_gram = lax.all_to_all(gram.reshape(nb, gram_rows * half), "blk", 0, 0, tiled=True)
    gram_part = obs_butterfly(jnp.sum(got_gram, axis=0))
    spread = jnp.broadcast_to(gram_part[None, :], (nb, gram_rows * half))
    square = lax.all_to_all(spread, "blk", 0, 0, tiled=True).reshape(panel_cols, half)
    diag = jnp.arange(half, dtype=jnp.int32)
    square = square + jnp.where(
        diag[None, :] == jnp.arange(panel_cols, dtype=jnp.int32)[:, None], prior_weight[None, :half], 0.0
    )

    parts = []
    for chunk in range(SPLIT):
        rows = pl_slice(chunk, CAP // SPLIT)
        payload = jnp.concatenate(
            [
                tile_rows[:, rows].reshape(nb, -1),
                panel_rows[:, rows].reshape(nb, -1),
            ],
            axis=1,
        )
        parts.append(lax.all_to_all(payload, "blk", 0, 0, tiled=True))
    owned = 0.0
    for chunk, got in enumerate(parts):
        width = CAP // SPLIT
        got_tiles = got[:, : width * bw].reshape(nb * width, bw)
        got_panel = got[:, width * bw :].reshape(nb * width, panel_cols)
        owned = owned + jnp.einsum("si,sp->ip", got_tiles, got_panel, precision=HI)
    owned = obs_butterfly(owned)

    my_block = jnp.sum(jnp.where(block_owner == my_j, block_range, 0))
    row_index = my_block * bw + jnp.arange(bw, dtype=jnp.int32)
    col_index = jnp.arange(panel_cols, dtype=jnp.int32)
    owned = owned + jnp.where(col_index[None, :] == row_index[:, None], prior_weight[None, :], 0.0)

    top = square[:half]
    mirrored = 0.5 * (top + top.T)
    factor = jnp.linalg.cholesky(mirrored)
    coupling = back_solve(factor, square[half:])
    first_rows = back_solve(factor, owned[:, :half])
    update_rows = owned[:, half:] - jnp.dot(
        first_rows, coupling.T, precision=HI, preferred_element_type=jnp.float32
    )
    return (first_rows, update_rows)


def solution(mesh):
    in_specs = (P(("obs", "blk"), None, None), P(("obs", "blk"), None), P(("obs", "blk")), P(), P())
    out_specs = (P("blk", None), P("blk", None))
    return jax.shard_map(local, mesh=mesh, in_specs=in_specs, out_specs=out_specs, check_vma=False)
```

```python
import jax
import jax.numpy as jnp
from jax import lax
from jax.sharding import PartitionSpec as P

CAP = 24
HI = lax.Precision.HIGHEST
FIRST = 8


def back_solve(factor, right_rows):
    return jax.scipy.linalg.solve_triangular(factor, right_rows.T, lower=True).T


def select_columns(labels, design_tiles, wanted):
    touched = design_tiles.shape[1]
    columns = jnp.zeros(
        (design_tiles.shape[0], wanted.shape[0], design_tiles.shape[2]), jnp.float32
    )
    for entry in range(touched):
        hit = labels[:, entry, None] == wanted[None, :]
        columns = columns + jnp.where(hit[:, :, None], design_tiles[:, entry, None, :], 0.0)
    return columns.reshape(design_tiles.shape[0], wanted.shape[0] * design_tiles.shape[2])


def obs_butterfly(x):
    n = lax.axis_size("obs")
    step = 1
    while step < n:
        perm = [(i, i ^ step) for i in range(n)]
        x = x + lax.ppermute(x, "obs", perm)
        step *= 2
    return x


def local(design_tiles, block_ids, obs_weight, block_owner, prior_weight):
    n_obs, touched, bw = design_tiles.shape
    nblk = block_owner.shape[0]
    panel_cols = prior_weight.shape[0]
    half = panel_cols // 2
    panel_blocks = panel_cols // bw
    nb = lax.axis_size("blk")
    my_j = lax.axis_index("blk")
    block_range = jnp.arange(nblk, dtype=jnp.int32)
    dest_range = jnp.arange(nb, dtype=jnp.int32)

    inv_owner = jnp.sum(
        jnp.where(block_owner[None, :] == dest_range[:, None], block_range[None, :], 0), axis=1
    )
    slot_owner = jnp.sum(
        jnp.where(block_ids[:, :, None] == block_range[None, None, :], block_owner[None, None, :], 0),
        axis=2,
    )
    hit = slot_owner[:, :, None] == dest_range[None, None, :]
    touch = jnp.sum(hit.astype(jnp.int32), axis=1)
    cum = jnp.cumsum(touch, axis=0)
    rank_range = jnp.arange(CAP, dtype=jnp.int32)
    obs_sel = jnp.sum((cum[:, :, None] <= rank_range[None, None, :]).astype(jnp.int32), axis=0)
    valid = rank_range[None, :] < cum[-1][:, None]
    obs_sel = jnp.minimum(obs_sel, n_obs - 1)
    owners_sel = slot_owner[obs_sel]
    k_sel = jnp.sum(
        jnp.where(owners_sel == dest_range[:, None, None], jnp.arange(touched, dtype=jnp.int32), 0),
        axis=2,
    )
    flat_tiles = design_tiles.reshape(n_obs * touched, bw)
    tile_rows = flat_tiles[obs_sel * touched + k_sel]

    panel_design = select_columns(
        block_ids, design_tiles, jnp.arange(panel_blocks, dtype=jnp.int32)
    )
    weighted = panel_design * obs_weight[:, None]
    panel_rows = weighted[obs_sel]
    tile_rows = jnp.where(valid[:, :, None], tile_rows, 0.0)
    panel_rows = jnp.where(valid[:, :, None], panel_rows, 0.0)

    gram = jnp.einsum("op,oq->pq", weighted, panel_design[:, :half], precision=HI)
    gram_rows = panel_cols // nb
    gram_width = gram_rows * half

    def routed(lo, hi):
        return [tile_rows[:, lo:hi].reshape(nb, -1), panel_rows[:, lo:hi].reshape(nb, -1)]

    first_got = lax.all_to_all(
        jnp.concatenate(routed(0, FIRST) + [gram.reshape(nb, gram_width)], axis=1), "blk", 0, 0, tiled=True
    )
    gram_part = obs_butterfly(jnp.sum(first_got[:, FIRST * (bw + panel_cols) :], axis=0))
    spread = jnp.broadcast_to(gram_part[None, :], (nb, gram_width))
    square = lax.all_to_all(spread, "blk", 0, 0, tiled=True).reshape(panel_cols, half)
    second_got = lax.all_to_all(jnp.concatenate(routed(FIRST, CAP), axis=1), "blk", 0, 0, tiled=True)

    diag = jnp.arange(half, dtype=jnp.int32)
    square = square + jnp.where(
        diag[None, :] == jnp.arange(panel_cols, dtype=jnp.int32)[:, None], prior_weight[None, :half], 0.0
    )
    top = square[:half]
    mirrored = 0.5 * (top + top.T)
    factor = jnp.linalg.cholesky(mirrored)
    inverse = jax.scipy.linalg.solve_triangular(factor, jnp.eye(half, dtype=jnp.float32), lower=True)
    coupling = jnp.dot(square[half:], inverse.T, precision=HI, preferred_element_type=jnp.float32)

    def owned_part(got, width):
        got_tiles = got[:, : width * bw].reshape(nb * width, bw)
        got_panel = got[:, width * bw : width * (bw + panel_cols)].reshape(nb * width, panel_cols)
        return jnp.einsum("si,sp->ip", got_tiles, got_panel, precision=HI)

    owned = owned_part(first_got, FIRST) + owned_part(second_got, CAP - FIRST)
    owned = obs_butterfly(owned)

    my_block = jnp.sum(jnp.where(block_owner == my_j, block_range, 0))
    row_index = my_block * bw + jnp.arange(bw, dtype=jnp.int32)
    col_index = jnp.arange(panel_cols, dtype=jnp.int32)
    owned = owned + jnp.where(col_index[None, :] == row_index[:, None], prior_weight[None, :], 0.0)

    first_rows = jnp.dot(owned[:, :half], inverse.T, precision=HI, preferred_element_type=jnp.float32)
    update_rows = owned[:, half:] - jnp.dot(
        first_rows, coupling.T, precision=HI, preferred_element_type=jnp.float32
    )
    return (first_rows, update_rows)


def solution(mesh):
    in_specs = (P(("obs", "blk"), None, None), P(("obs", "blk"), None), P(("obs", "blk")), P(), P())
    out_specs = (P("blk", None), P("blk", None))
    return jax.shard_map(local, mesh=mesh, in_specs=in_specs, out_specs=out_specs, check_vma=False)
```

```python
import jax
import jax.numpy as jnp
from jax import lax
from jax.sharding import PartitionSpec as P

CAP = 24
HI = lax.Precision.HIGHEST
SPLIT = 2


def pl_slice(chunk, size):
    return slice(chunk * size, (chunk + 1) * size)


def dot(a, b):
    return jnp.dot(a, b, precision=HI, preferred_element_type=jnp.float32)


def factor_inverse(mirrored):
    n = mirrored.shape[0] // 2
    eye = jnp.eye(n, dtype=jnp.float32)
    low = jnp.linalg.cholesky(mirrored[:n, :n])
    low_inv = jax.scipy.linalg.solve_triangular(low, eye, lower=True)
    left = dot(mirrored[n:, :n], low_inv.T)
    high = jnp.linalg.cholesky(mirrored[n:, n:] - dot(left, left.T))
    high_inv = jax.scipy.linalg.solve_triangular(high, eye, lower=True)
    corner = -dot(high_inv, dot(left, low_inv))
    return jnp.concatenate(
        [jnp.concatenate([low_inv, jnp.zeros_like(low_inv)], axis=1), jnp.concatenate([corner, high_inv], axis=1)],
        axis=0,
    )


def select_columns(labels, design_tiles, wanted):
    touched = design_tiles.shape[1]
    columns = jnp.zeros(
        (design_tiles.shape[0], wanted.shape[0], design_tiles.shape[2]), jnp.float32
    )
    for entry in range(touched):
        hit = labels[:, entry, None] == wanted[None, :]
        columns = columns + jnp.where(hit[:, :, None], design_tiles[:, entry, None, :], 0.0)
    return columns.reshape(design_tiles.shape[0], wanted.shape[0] * design_tiles.shape[2])


def obs_butterfly(x):
    n = lax.axis_size("obs")
    step = 1
    while step < n:
        perm = [(i, i ^ step) for i in range(n)]
        x = x + lax.ppermute(x, "obs", perm)
        step *= 2
    return x


def local(design_tiles, block_ids, obs_weight, block_owner, prior_weight):
    n_obs, touched, bw = design_tiles.shape
    nblk = block_owner.shape[0]
    panel_cols = prior_weight.shape[0]
    half = panel_cols // 2
    panel_blocks = panel_cols // bw
    nb = lax.axis_size("blk")
    my_j = lax.axis_index("blk")
    block_range = jnp.arange(nblk, dtype=jnp.int32)
    dest_range = jnp.arange(nb, dtype=jnp.int32)

    inv_owner = jnp.sum(
        jnp.where(block_owner[None, :] == dest_range[:, None], block_range[None, :], 0), axis=1
    )
    slot_owner = jnp.sum(
        jnp.where(block_ids[:, :, None] == block_range[None, None, :], block_owner[None, None, :], 0),
        axis=2,
    )
    hit = slot_owner[:, :, None] == dest_range[None, None, :]
    touch = jnp.sum(hit.astype(jnp.int32), axis=1)
    cum = jnp.cumsum(touch, axis=0)
    rank_range = jnp.arange(CAP, dtype=jnp.int32)
    obs_sel = jnp.sum((cum[:, :, None] <= rank_range[None, None, :]).astype(jnp.int32), axis=0)
    valid = rank_range[None, :] < cum[-1][:, None]
    obs_sel = jnp.minimum(obs_sel, n_obs - 1)
    owners_sel = slot_owner[obs_sel]
    k_sel = jnp.sum(
        jnp.where(owners_sel == dest_range[:, None, None], jnp.arange(touched, dtype=jnp.int32), 0),
        axis=2,
    )
    flat_tiles = design_tiles.reshape(n_obs * touched, bw)
    tile_rows = flat_tiles[obs_sel * touched + k_sel]

    panel_design = select_columns(
        block_ids, design_tiles, jnp.arange(panel_blocks, dtype=jnp.int32)
    )
    weighted = panel_design * obs_weight[:, None]
    panel_rows = weighted[obs_sel]
    tile_rows = jnp.where(valid[:, :, None], tile_rows, 0.0)
    panel_rows = jnp.where(valid[:, :, None], panel_rows, 0.0)

    gram = jnp.einsum("op,oq->pq", weighted, panel_design[:, :half], precision=HI)
    gram_rows = panel_cols // nb
    got_gram = lax.all_to_all(gram.reshape(nb, gram_rows * half), "blk", 0, 0, tiled=True)
    gram_part = obs_butterfly(jnp.sum(got_gram, axis=0))
    spread = jnp.broadcast_to(gram_part[None, :], (nb, gram_rows * half))
    square = lax.all_to_all(spread, "blk", 0, 0, tiled=True).reshape(panel_cols, half)
    diag = jnp.arange(half, dtype=jnp.int32)
    square = square + jnp.where(
        diag[None, :] == jnp.arange(panel_cols, dtype=jnp.int32)[:, None], prior_weight[None, :half], 0.0
    )

    parts = []
    for chunk in range(SPLIT):
        rows = pl_slice(chunk, CAP // SPLIT)
        payload = jnp.concatenate(
            [
                tile_rows[:, rows].reshape(nb, -1),
                panel_rows[:, rows].reshape(nb, -1),
            ],
            axis=1,
        )
        parts.append(lax.all_to_all(payload, "blk", 0, 0, tiled=True))
    owned = 0.0
    for chunk, got in enumerate(parts):
        width = CAP // SPLIT
        got_tiles = got[:, : width * bw].reshape(nb * width, bw)
        got_panel = got[:, width * bw :].reshape(nb * width, panel_cols)
        owned = owned + jnp.einsum("si,sp->ip", got_tiles, got_panel, precision=HI)
    owned = obs_butterfly(owned)

    my_block = jnp.sum(jnp.where(block_owner == my_j, block_range, 0))
    row_index = my_block * bw + jnp.arange(bw, dtype=jnp.int32)
    col_index = jnp.arange(panel_cols, dtype=jnp.int32)
    owned = owned + jnp.where(col_index[None, :] == row_index[:, None], prior_weight[None, :], 0.0)

    inverse = factor_inverse(0.5 * (square[:half] + square[:half].T))
    coupling = jnp.dot(square[half:], inverse.T, precision=HI, preferred_element_type=jnp.float32)
    first_rows = jnp.dot(owned[:, :half], inverse.T, precision=HI, preferred_element_type=jnp.float32)
    update_rows = owned[:, half:] - jnp.dot(
        first_rows, coupling.T, precision=HI, preferred_element_type=jnp.float32
    )
    return (first_rows, update_rows)


def solution(mesh):
    in_specs = (P(("obs", "blk"), None, None), P(("obs", "blk"), None), P(("obs", "blk")), P(), P())
    out_specs = (P("blk", None), P("blk", None))
    return jax.shard_map(local, mesh=mesh, in_specs=in_specs, out_specs=out_specs, check_vma=False)
```

```python
import jax
import jax.numpy as jnp
from jax import lax
from jax.sharding import PartitionSpec as P

CAP = 24
HI = lax.Precision.HIGHEST
FIRST = 8


def dot(a, b):
    return jnp.dot(a, b, precision=HI, preferred_element_type=jnp.float32)


def factor_inverse(mirrored):
    n = mirrored.shape[0] // 2
    eye = jnp.eye(n, dtype=jnp.float32)
    low = jnp.linalg.cholesky(mirrored[:n, :n])
    low_inv = jax.scipy.linalg.solve_triangular(low, eye, lower=True)
    left = dot(mirrored[n:, :n], low_inv.T)
    high = jnp.linalg.cholesky(mirrored[n:, n:] - dot(left, left.T))
    high_inv = jax.scipy.linalg.solve_triangular(high, eye, lower=True)
    corner = -dot(high_inv, dot(left, low_inv))
    return jnp.concatenate(
        [jnp.concatenate([low_inv, jnp.zeros_like(low_inv)], axis=1), jnp.concatenate([corner, high_inv], axis=1)],
        axis=0,
    )


def select_columns(labels, design_tiles, wanted):
    touched = design_tiles.shape[1]
    columns = jnp.zeros(
        (design_tiles.shape[0], wanted.shape[0], design_tiles.shape[2]), jnp.float32
    )
    for entry in range(touched):
        hit = labels[:, entry, None] == wanted[None, :]
        columns = columns + jnp.where(hit[:, :, None], design_tiles[:, entry, None, :], 0.0)
    return columns.reshape(design_tiles.shape[0], wanted.shape[0] * design_tiles.shape[2])


def butterfly(x, axis):
    n = lax.axis_size(axis)
    step = 1
    while step < n:
        perm = [(i, i ^ step) for i in range(n)]
        x = x + lax.ppermute(x, axis, perm)
        step *= 2
    return x


def local(design_tiles, block_ids, obs_weight, block_owner, prior_weight):
    n_obs, touched, bw = design_tiles.shape
    nblk = block_owner.shape[0]
    panel_cols = prior_weight.shape[0]
    half = panel_cols // 2
    panel_blocks = panel_cols // bw
    nb = lax.axis_size("blk")
    my_j = lax.axis_index("blk")
    block_range = jnp.arange(nblk, dtype=jnp.int32)
    dest_range = jnp.arange(nb, dtype=jnp.int32)

    inv_owner = jnp.sum(
        jnp.where(block_owner[None, :] == dest_range[:, None], block_range[None, :], 0), axis=1
    )
    slot_owner = jnp.sum(
        jnp.where(block_ids[:, :, None] == block_range[None, None, :], block_owner[None, None, :], 0),
        axis=2,
    )
    hit = slot_owner[:, :, None] == dest_range[None, None, :]
    touch = jnp.sum(hit.astype(jnp.int32), axis=1)
    cum = jnp.cumsum(touch, axis=0)
    rank_range = jnp.arange(CAP, dtype=jnp.int32)
    obs_sel = jnp.sum((cum[:, :, None] <= rank_range[None, None, :]).astype(jnp.int32), axis=0)
    valid = rank_range[None, :] < cum[-1][:, None]
    obs_sel = jnp.minimum(obs_sel, n_obs - 1)
    owners_sel = slot_owner[obs_sel]
    k_sel = jnp.sum(
        jnp.where(owners_sel == dest_range[:, None, None], jnp.arange(touched, dtype=jnp.int32), 0),
        axis=2,
    )
    flat_tiles = design_tiles.reshape(n_obs * touched, bw)
    tile_rows = flat_tiles[obs_sel * touched + k_sel]

    panel_design = select_columns(
        block_ids, design_tiles, jnp.arange(panel_blocks, dtype=jnp.int32)
    )
    weighted = panel_design * obs_weight[:, None]
    panel_rows = weighted[obs_sel]
    tile_rows = jnp.where(valid[:, :, None], tile_rows, 0.0)
    panel_rows = jnp.where(valid[:, :, None], panel_rows, 0.0)

    gram = jnp.einsum("op,oq->pq", weighted, panel_design[:, :half], precision=HI)
    square = butterfly(butterfly(gram, "obs"), "blk")
    diag = jnp.arange(half, dtype=jnp.int32)
    square = square + jnp.where(
        diag[None, :] == jnp.arange(panel_cols, dtype=jnp.int32)[:, None], prior_weight[None, :half], 0.0
    )

    owned = 0.0
    for lo, hi in ((0, FIRST), (FIRST, CAP)):
        payload = jnp.concatenate([tile_rows[:, lo:hi], panel_rows[:, lo:hi]], axis=2)
        got = lax.all_to_all(payload, "blk", 0, 0, tiled=True).reshape(nb * (hi - lo), bw + panel_cols)
        owned = owned + jnp.einsum("si,sp->ip", got[:, :bw], got[:, bw:], precision=HI)
    owned = butterfly(owned, "obs")

    my_block = jnp.sum(jnp.where(block_owner == my_j, block_range, 0))
    row_index = my_block * bw + jnp.arange(bw, dtype=jnp.int32)
    col_index = jnp.arange(panel_cols, dtype=jnp.int32)
    owned = owned + jnp.where(col_index[None, :] == row_index[:, None], prior_weight[None, :], 0.0)

    inverse = factor_inverse(0.5 * (square[:half] + square[:half].T))
    coupling = jnp.dot(square[half:], inverse.T, precision=HI, preferred_element_type=jnp.float32)
    first_rows = jnp.dot(owned[:, :half], inverse.T, precision=HI, preferred_element_type=jnp.float32)
    update_rows = owned[:, half:] - jnp.dot(
        first_rows, coupling.T, precision=HI, preferred_element_type=jnp.float32
    )
    return (first_rows, update_rows)


def solution(mesh):
    in_specs = (P(("obs", "blk"), None, None), P(("obs", "blk"), None), P(("obs", "blk")), P(), P())
    out_specs = (P("blk", None), P("blk", None))
    return jax.shard_map(local, mesh=mesh, in_specs=in_specs, out_specs=out_specs, check_vma=False)
```

```python
import jax
import jax.numpy as jnp
from jax import lax
from jax.sharding import PartitionSpec as P

CAP = 24
HI = lax.Precision.HIGHEST
FIRST = 8


def dot(a, b):
    return jnp.dot(a, b, precision=HI, preferred_element_type=jnp.float32)


def factor_inverse(mirrored):
    n = mirrored.shape[0] // 2
    eye = jnp.eye(n, dtype=jnp.float32)
    low = jnp.linalg.cholesky(mirrored[:n, :n])
    low_inv = jax.scipy.linalg.solve_triangular(low, eye, lower=True)
    left = dot(mirrored[n:, :n], low_inv.T)
    high = jnp.linalg.cholesky(mirrored[n:, n:] - dot(left, left.T))
    high_inv = jax.scipy.linalg.solve_triangular(high, eye, lower=True)
    corner = -dot(high_inv, dot(left, low_inv))
    return jnp.concatenate(
        [jnp.concatenate([low_inv, jnp.zeros_like(low_inv)], axis=1), jnp.concatenate([corner, high_inv], axis=1)],
        axis=0,
    )


def select_columns(labels, design_tiles, wanted):
    touched = design_tiles.shape[1]
    columns = jnp.zeros(
        (design_tiles.shape[0], wanted.shape[0], design_tiles.shape[2]), jnp.float32
    )
    for entry in range(touched):
        hit = labels[:, entry, None] == wanted[None, :]
        columns = columns + jnp.where(hit[:, :, None], design_tiles[:, entry, None, :], 0.0)
    return columns.reshape(design_tiles.shape[0], wanted.shape[0] * design_tiles.shape[2])


def obs_butterfly(x):
    n = lax.axis_size("obs")
    step = 1
    while step < n:
        perm = [(i, i ^ step) for i in range(n)]
        x = x + lax.ppermute(x, "obs", perm)
        step *= 2
    return x


def local(design_tiles, block_ids, obs_weight, block_owner, prior_weight):
    n_obs, touched, bw = design_tiles.shape
    nblk = block_owner.shape[0]
    panel_cols = prior_weight.shape[0]
    half = panel_cols // 2
    panel_blocks = panel_cols // bw
    nb = lax.axis_size("blk")
    my_j = lax.axis_index("blk")
    block_range = jnp.arange(nblk, dtype=jnp.int32)
    dest_range = jnp.arange(nb, dtype=jnp.int32)

    inv_owner = jnp.sum(
        jnp.where(block_owner[None, :] == dest_range[:, None], block_range[None, :], 0), axis=1
    )
    slot_owner = jnp.sum(
        jnp.where(block_ids[:, :, None] == block_range[None, None, :], block_owner[None, None, :], 0),
        axis=2,
    )
    hit = slot_owner[:, :, None] == dest_range[None, None, :]
    touch = jnp.sum(hit.astype(jnp.int32), axis=1)
    cum = jnp.cumsum(touch, axis=0)
    rank_range = jnp.arange(CAP, dtype=jnp.int32)
    obs_sel = jnp.sum((cum[:, :, None] <= rank_range[None, None, :]).astype(jnp.int32), axis=0)
    valid = rank_range[None, :] < cum[-1][:, None]
    obs_sel = jnp.minimum(obs_sel, n_obs - 1)
    owners_sel = slot_owner[obs_sel]
    k_sel = jnp.sum(
        jnp.where(owners_sel == dest_range[:, None, None], jnp.arange(touched, dtype=jnp.int32), 0),
        axis=2,
    )
    flat_tiles = design_tiles.reshape(n_obs * touched, bw)
    tile_rows = flat_tiles[obs_sel * touched + k_sel]

    panel_design = select_columns(
        block_ids, design_tiles, jnp.arange(panel_blocks, dtype=jnp.int32)
    )
    weighted = panel_design * obs_weight[:, None]
    panel_rows = weighted[obs_sel]
    tile_rows = jnp.where(valid[:, :, None], tile_rows, 0.0)
    panel_rows = jnp.where(valid[:, :, None], panel_rows, 0.0)

    gram = jnp.einsum("op,oq->pq", weighted, panel_design[:, :half], precision=HI)
    gram_rows = panel_cols // nb
    got_gram = lax.all_to_all(gram.reshape(nb, gram_rows, half), "blk", 0, 0, tiled=True)
    gram_part = obs_butterfly(jnp.sum(got_gram, axis=0))
    spread = jnp.broadcast_to(gram_part[None], (nb, gram_rows, half))
    square = lax.all_to_all(spread, "blk", 0, 0, tiled=True).reshape(panel_cols, half)
    diag = jnp.arange(half, dtype=jnp.int32)
    square = square + jnp.where(
        diag[None, :] == jnp.arange(panel_cols, dtype=jnp.int32)[:, None], prior_weight[None, :half], 0.0
    )

    owned = 0.0
    for lo, hi in ((0, FIRST), (FIRST, CAP)):
        payload = jnp.concatenate([tile_rows[:, lo:hi], panel_rows[:, lo:hi]], axis=2)
        got = lax.all_to_all(payload, "blk", 0, 0, tiled=True).reshape(nb * (hi - lo), bw + panel_cols)
        owned = owned + jnp.einsum("si,sp->ip", got[:, :bw], got[:, bw:], precision=HI)
    owned = obs_butterfly(owned)

    my_block = jnp.sum(jnp.where(block_owner == my_j, block_range, 0))
    row_index = my_block * bw + jnp.arange(bw, dtype=jnp.int32)
    col_index = jnp.arange(panel_cols, dtype=jnp.int32)
    owned = owned + jnp.where(col_index[None, :] == row_index[:, None], prior_weight[None, :], 0.0)

    inverse = factor_inverse(0.5 * (square[:half] + square[:half].T))
    coupling = jnp.dot(square[half:], inverse.T, precision=HI, preferred_element_type=jnp.float32)
    first_rows = jnp.dot(owned[:, :half], inverse.T, precision=HI, preferred_element_type=jnp.float32)
    update_rows = owned[:, half:] - jnp.dot(
        first_rows, coupling.T, precision=HI, preferred_element_type=jnp.float32
    )
    return (first_rows, update_rows)


def solution(mesh):
    in_specs = (P(("obs", "blk"), None, None), P(("obs", "blk"), None), P(("obs", "blk")), P(), P())
    out_specs = (P("blk", None), P("blk", None))
    return jax.shard_map(local, mesh=mesh, in_specs=in_specs, out_specs=out_specs, check_vma=False)
```

```python
import jax
import jax.numpy as jnp
from jax import lax
from jax.sharding import PartitionSpec as P

CAP = 24
HI = lax.Precision.HIGHEST
FIRST = 8


def dot(a, b):
    return jnp.dot(a, b, precision=HI, preferred_element_type=jnp.float32)


def factor_inverse(mirrored):
    n = mirrored.shape[0] // 2
    eye = jnp.eye(n, dtype=jnp.float32)
    low = jnp.linalg.cholesky(mirrored[:n, :n])
    low_inv = jax.scipy.linalg.solve_triangular(low, eye, lower=True)
    left = dot(mirrored[n:, :n], low_inv.T)
    high = jnp.linalg.cholesky(mirrored[n:, n:] - dot(left, left.T))
    high_inv = jax.scipy.linalg.solve_triangular(high, eye, lower=True)
    corner = -dot(high_inv, dot(left, low_inv))
    return jnp.concatenate(
        [jnp.concatenate([low_inv, jnp.zeros_like(low_inv)], axis=1), jnp.concatenate([corner, high_inv], axis=1)],
        axis=0,
    )


def select_columns(labels, design_tiles, wanted):
    touched = design_tiles.shape[1]
    columns = jnp.zeros(
        (design_tiles.shape[0], wanted.shape[0], design_tiles.shape[2]), jnp.float32
    )
    for entry in range(touched):
        hit = labels[:, entry, None] == wanted[None, :]
        columns = columns + jnp.where(hit[:, :, None], design_tiles[:, entry, None, :], 0.0)
    return columns.reshape(design_tiles.shape[0], wanted.shape[0] * design_tiles.shape[2])


def obs_butterfly(x):
    n = lax.axis_size("obs")
    step = 1
    while step < n:
        perm = [(i, i ^ step) for i in range(n)]
        x = x + lax.ppermute(x, "obs", perm)
        step *= 2
    return x


def local(design_tiles, block_ids, obs_weight, block_owner, prior_weight):
    n_obs, touched, bw = design_tiles.shape
    nblk = block_owner.shape[0]
    panel_cols = prior_weight.shape[0]
    half = panel_cols // 2
    panel_blocks = panel_cols // bw
    nb = lax.axis_size("blk")
    my_j = lax.axis_index("blk")
    block_range = jnp.arange(nblk, dtype=jnp.int32)
    dest_range = jnp.arange(nb, dtype=jnp.int32)

    inv_owner = jnp.sum(
        jnp.where(block_owner[None, :] == dest_range[:, None], block_range[None, :], 0), axis=1
    )
    slot_owner = jnp.sum(
        jnp.where(block_ids[:, :, None] == block_range[None, None, :], block_owner[None, None, :], 0),
        axis=2,
    )
    hit = slot_owner[:, :, None] == dest_range[None, None, :]
    touch = jnp.sum(hit.astype(jnp.int32), axis=1)
    cum = jnp.cumsum(touch, axis=0)
    rank_range = jnp.arange(CAP, dtype=jnp.int32)
    obs_sel = jnp.sum((cum[:, :, None] <= rank_range[None, None, :]).astype(jnp.int32), axis=0)
    valid = rank_range[None, :] < cum[-1][:, None]
    obs_sel = jnp.minimum(obs_sel, n_obs - 1)
    owners_sel = slot_owner[obs_sel]
    k_sel = jnp.sum(
        jnp.where(owners_sel == dest_range[:, None, None], jnp.arange(touched, dtype=jnp.int32), 0),
        axis=2,
    )
    flat_tiles = design_tiles.reshape(n_obs * touched, bw)
    tile_rows = flat_tiles[obs_sel * touched + k_sel]

    panel_design = select_columns(
        block_ids, design_tiles, jnp.arange(panel_blocks, dtype=jnp.int32)
    )
    weighted = panel_design * obs_weight[:, None]
    panel_rows = weighted[obs_sel]
    tile_rows = jnp.where(valid[:, :, None], tile_rows, 0.0)
    panel_rows = jnp.where(valid[:, :, None], panel_rows, 0.0)

    gram = jnp.einsum("op,oq->pq", weighted, panel_design[:, :half], precision=HI)
    gram_rows = panel_cols // nb
    got_gram = lax.all_to_all(gram.reshape(nb, gram_rows, half), "blk", 0, 0, tiled=True)
    gram_part = obs_butterfly(jnp.sum(got_gram, axis=0))
    spread = jnp.broadcast_to(gram_part[None], (nb, gram_rows, half))

    def routed(lo, hi):
        return [tile_rows[:, lo:hi], panel_rows[:, lo:hi]]

    def owned_part(got):
        got = got.reshape(-1, bw + panel_cols)
        return jnp.einsum("si,sp->ip", got[:, :bw], got[:, bw:], precision=HI)

    mixed = lax.all_to_all(jnp.concatenate([spread] + routed(0, FIRST), axis=2), "blk", 0, 0, tiled=True)
    square = mixed[:, :, :half].reshape(panel_cols, half)
    owned = owned_part(mixed[:, :, half:])
    rest = lax.all_to_all(jnp.concatenate(routed(FIRST, CAP), axis=2), "blk", 0, 0, tiled=True)
    owned = owned + owned_part(rest)
    diag = jnp.arange(half, dtype=jnp.int32)
    square = square + jnp.where(
        diag[None, :] == jnp.arange(panel_cols, dtype=jnp.int32)[:, None], prior_weight[None, :half], 0.0
    )
    owned = obs_butterfly(owned)

    my_block = jnp.sum(jnp.where(block_owner == my_j, block_range, 0))
    row_index = my_block * bw + jnp.arange(bw, dtype=jnp.int32)
    col_index = jnp.arange(panel_cols, dtype=jnp.int32)
    owned = owned + jnp.where(col_index[None, :] == row_index[:, None], prior_weight[None, :], 0.0)

    inverse = factor_inverse(0.5 * (square[:half] + square[:half].T))
    coupling = jnp.dot(square[half:], inverse.T, precision=HI, preferred_element_type=jnp.float32)
    first_rows = jnp.dot(owned[:, :half], inverse.T, precision=HI, preferred_element_type=jnp.float32)
    update_rows = owned[:, half:] - jnp.dot(
        first_rows, coupling.T, precision=HI, preferred_element_type=jnp.float32
    )
    return (first_rows, update_rows)


def solution(mesh):
    in_specs = (P(("obs", "blk"), None, None), P(("obs", "blk"), None), P(("obs", "blk")), P(), P())
    out_specs = (P("blk", None), P("blk", None))
    return jax.shard_map(local, mesh=mesh, in_specs=in_specs, out_specs=out_specs, check_vma=False)
```

```python
import jax
import jax.numpy as jnp
from jax import lax
from jax.sharding import PartitionSpec as P

CAP = 24
HI = lax.Precision.HIGHEST
FIRST = 8


def dot(a, b):
    return jnp.dot(a, b, precision=HI, preferred_element_type=jnp.float32)


def factor_inverse(mirrored):
    n = mirrored.shape[0] // 2
    eye = jnp.eye(n, dtype=jnp.float32)
    low = jnp.linalg.cholesky(mirrored[:n, :n])
    low_inv = jax.scipy.linalg.solve_triangular(low, eye, lower=True)
    left = dot(mirrored[n:, :n], low_inv.T)
    high = jnp.linalg.cholesky(mirrored[n:, n:] - dot(left, left.T))
    high_inv = jax.scipy.linalg.solve_triangular(high, eye, lower=True)
    corner = -dot(high_inv, dot(left, low_inv))
    return jnp.concatenate(
        [jnp.concatenate([low_inv, jnp.zeros_like(low_inv)], axis=1), jnp.concatenate([corner, high_inv], axis=1)],
        axis=0,
    )


def select_columns(labels, design_tiles, wanted):
    touched = design_tiles.shape[1]
    columns = jnp.zeros(
        (design_tiles.shape[0], wanted.shape[0], design_tiles.shape[2]), jnp.float32
    )
    for entry in range(touched):
        hit = labels[:, entry, None] == wanted[None, :]
        columns = columns + jnp.where(hit[:, :, None], design_tiles[:, entry, None, :], 0.0)
    return columns.reshape(design_tiles.shape[0], wanted.shape[0] * design_tiles.shape[2])


def obs_butterfly(x):
    n = lax.axis_size("obs")
    me = lax.axis_index("obs")
    got = [x] + [lax.ppermute(x, "obs", [(i, (i + s) % n) for i in range(n)]) for s in range(1, n)]
    ordered = jnp.stack(got)
    parts = [ordered[(me - src) % n] for src in range(n)]
    while len(parts) > 1:
        parts = [parts[i] + parts[i + 1] for i in range(0, len(parts), 2)]
    return parts[0]


def local(design_tiles, block_ids, obs_weight, block_owner, prior_weight):
    n_obs, touched, bw = design_tiles.shape
    nblk = block_owner.shape[0]
    panel_cols = prior_weight.shape[0]
    half = panel_cols // 2
    panel_blocks = panel_cols // bw
    nb = lax.axis_size("blk")
    my_j = lax.axis_index("blk")
    block_range = jnp.arange(nblk, dtype=jnp.int32)
    dest_range = jnp.arange(nb, dtype=jnp.int32)

    inv_owner = jnp.sum(
        jnp.where(block_owner[None, :] == dest_range[:, None], block_range[None, :], 0), axis=1
    )
    slot_owner = jnp.sum(
        jnp.where(block_ids[:, :, None] == block_range[None, None, :], block_owner[None, None, :], 0),
        axis=2,
    )
    hit = slot_owner[:, :, None] == dest_range[None, None, :]
    touch = jnp.sum(hit.astype(jnp.int32), axis=1)
    cum = jnp.cumsum(touch, axis=0)
    rank_range = jnp.arange(CAP, dtype=jnp.int32)
    obs_sel = jnp.sum((cum[:, :, None] <= rank_range[None, None, :]).astype(jnp.int32), axis=0)
    valid = rank_range[None, :] < cum[-1][:, None]
    obs_sel = jnp.minimum(obs_sel, n_obs - 1)
    owners_sel = slot_owner[obs_sel]
    k_sel = jnp.sum(
        jnp.where(owners_sel == dest_range[:, None, None], jnp.arange(touched, dtype=jnp.int32), 0),
        axis=2,
    )
    flat_tiles = design_tiles.reshape(n_obs * touched, bw)
    tile_rows = flat_tiles[obs_sel * touched + k_sel]

    panel_design = select_columns(
        block_ids, design_tiles, jnp.arange(panel_blocks, dtype=jnp.int32)
    )
    weighted = panel_design * obs_weight[:, None]
    panel_rows = weighted[obs_sel]
    tile_rows = jnp.where(valid[:, :, None], tile_rows, 0.0)
    panel_rows = jnp.where(valid[:, :, None], panel_rows, 0.0)

    gram = jnp.einsum("op,oq->pq", weighted, panel_design[:, :half], precision=HI)
    gram_rows = panel_cols // nb
    got_gram = lax.all_to_all(gram.reshape(nb, gram_rows, half), "blk", 0, 0, tiled=True)
    gram_part = obs_butterfly(jnp.sum(got_gram, axis=0))
    spread = jnp.broadcast_to(gram_part[None], (nb, gram_rows, half))

    def routed(lo, hi):
        return [tile_rows[:, lo:hi], panel_rows[:, lo:hi]]

    def owned_part(got):
        got = got.reshape(-1, bw + panel_cols)
        return jnp.einsum("si,sp->ip", got[:, :bw], got[:, bw:], precision=HI)

    mixed = lax.all_to_all(jnp.concatenate([spread] + routed(0, FIRST), axis=2), "blk", 0, 0, tiled=True)
    square = mixed[:, :, :half].reshape(panel_cols, half)
    owned = owned_part(mixed[:, :, half:])
    rest = lax.all_to_all(jnp.concatenate(routed(FIRST, CAP), axis=2), "blk", 0, 0, tiled=True)
    owned = owned + owned_part(rest)
    diag = jnp.arange(half, dtype=jnp.int32)
    square = square + jnp.where(
        diag[None, :] == jnp.arange(panel_cols, dtype=jnp.int32)[:, None], prior_weight[None, :half], 0.0
    )
    owned = obs_butterfly(owned)

    my_block = jnp.sum(jnp.where(block_owner == my_j, block_range, 0))
    row_index = my_block * bw + jnp.arange(bw, dtype=jnp.int32)
    col_index = jnp.arange(panel_cols, dtype=jnp.int32)
    owned = owned + jnp.where(col_index[None, :] == row_index[:, None], prior_weight[None, :], 0.0)

    inverse = factor_inverse(0.5 * (square[:half] + square[:half].T))
    coupling = jnp.dot(square[half:], inverse.T, precision=HI, preferred_element_type=jnp.float32)
    first_rows = jnp.dot(owned[:, :half], inverse.T, precision=HI, preferred_element_type=jnp.float32)
    update_rows = owned[:, half:] - jnp.dot(
        first_rows, coupling.T, precision=HI, preferred_element_type=jnp.float32
    )
    return (first_rows, update_rows)


def solution(mesh):
    in_specs = (P(("obs", "blk"), None, None), P(("obs", "blk"), None), P(("obs", "blk")), P(), P())
    out_specs = (P("blk", None), P("blk", None))
    return jax.shard_map(local, mesh=mesh, in_specs=in_specs, out_specs=out_specs, check_vma=False)
```

```python
import jax
import jax.numpy as jnp
from jax import lax
from jax.sharding import PartitionSpec as P

CAP = 24
HI = lax.Precision.HIGHEST
FIRST = 8


def dot(a, b):
    return jnp.dot(a, b, precision=HI, preferred_element_type=jnp.float32)


def factor_inverse(mirrored):
    n = mirrored.shape[0] // 2
    eye = jnp.eye(n, dtype=jnp.float32)
    low = jnp.linalg.cholesky(mirrored[:n, :n])
    low_inv = jax.scipy.linalg.solve_triangular(low, eye, lower=True)
    left = dot(mirrored[n:, :n], low_inv.T)
    high = jnp.linalg.cholesky(mirrored[n:, n:] - dot(left, left.T))
    high_inv = jax.scipy.linalg.solve_triangular(high, eye, lower=True)
    corner = -dot(high_inv, dot(left, low_inv))
    return jnp.concatenate(
        [jnp.concatenate([low_inv, jnp.zeros_like(low_inv)], axis=1), jnp.concatenate([corner, high_inv], axis=1)],
        axis=0,
    )


def select_columns(labels, design_tiles, wanted):
    touched = design_tiles.shape[1]
    columns = jnp.zeros(
        (design_tiles.shape[0], wanted.shape[0], design_tiles.shape[2]), jnp.float32
    )
    for entry in range(touched):
        hit = labels[:, entry, None] == wanted[None, :]
        columns = columns + jnp.where(hit[:, :, None], design_tiles[:, entry, None, :], 0.0)
    return columns.reshape(design_tiles.shape[0], wanted.shape[0] * design_tiles.shape[2])


def obs_butterfly(x):
    n = lax.axis_size("obs")
    step = 1
    while step < n:
        perm = [(i, i ^ step) for i in range(n)]
        x = x + lax.ppermute(x, "obs", perm)
        step *= 2
    return x


def local(design_tiles, block_ids, obs_weight, block_owner, prior_weight):
    n_obs, touched, bw = design_tiles.shape
    nblk = block_owner.shape[0]
    panel_cols = prior_weight.shape[0]
    half = panel_cols // 2
    panel_blocks = panel_cols // bw
    nb = lax.axis_size("blk")
    my_j = lax.axis_index("blk")
    block_range = jnp.arange(nblk, dtype=jnp.int32)
    dest_range = jnp.arange(nb, dtype=jnp.int32)

    inv_owner = jnp.sum(
        jnp.where(block_owner[None, :] == dest_range[:, None], block_range[None, :], 0), axis=1
    )
    slot_owner = jnp.sum(
        jnp.where(block_ids[:, :, None] == block_range[None, None, :], block_owner[None, None, :], 0),
        axis=2,
    )
    hit = slot_owner[:, :, None] == dest_range[None, None, :]
    touch = jnp.sum(hit.astype(jnp.int32), axis=1)
    cum = jnp.cumsum(touch, axis=0)
    rank_range = jnp.arange(CAP, dtype=jnp.int32)
    obs_sel = jnp.sum((cum[:, :, None] <= rank_range[None, None, :]).astype(jnp.int32), axis=0)
    valid = rank_range[None, :] < cum[-1][:, None]
    obs_sel = jnp.minimum(obs_sel, n_obs - 1)
    owners_sel = slot_owner[obs_sel]
    k_sel = jnp.sum(
        jnp.where(owners_sel == dest_range[:, None, None], jnp.arange(touched, dtype=jnp.int32), 0),
        axis=2,
    )
    flat_tiles = design_tiles.reshape(n_obs * touched, bw)
    tile_rows = flat_tiles[obs_sel * touched + k_sel]

    panel_design = select_columns(
        block_ids, design_tiles, jnp.arange(panel_blocks, dtype=jnp.int32)
    )
    weighted = panel_design * obs_weight[:, None]
    panel_rows = weighted[obs_sel]
    tile_rows = jnp.where(valid[:, :, None], tile_rows, 0.0)
    panel_rows = jnp.where(valid[:, :, None], panel_rows, 0.0)

    gram = jnp.einsum("op,oq->pq", weighted, panel_design[:, :half], precision=HI)
    gram_rows = panel_cols // nb
    got_gram = lax.all_to_all(gram.reshape(nb, gram_rows, half), "blk", 0, 0, tiled=True)
    gram_part = obs_butterfly(jnp.sum(got_gram, axis=0))
    spread = jnp.broadcast_to(gram_part[None], (nb, gram_rows, half))

    def routed(lo, hi):
        return [tile_rows[:, lo:hi], panel_rows[:, lo:hi]]

    def owned_part(got):
        got = got.reshape(-1, bw + panel_cols)
        return jnp.einsum("si,sp->ip", got[:, :bw], got[:, bw:], precision=HI)

    mixed = lax.all_to_all(jnp.concatenate([spread] + routed(0, FIRST), axis=2), "blk", 0, 0, tiled=True)
    square = mixed[:, :, :half].reshape(panel_cols, half)
    owned = owned_part(mixed[:, :, half:])
    rest = lax.all_to_all(jnp.concatenate(routed(FIRST, CAP), axis=2), "blk", 0, 0, tiled=True)
    owned = owned + owned_part(rest)
    diag = jnp.arange(half, dtype=jnp.int32)
    square = square + jnp.where(
        diag[None, :] == jnp.arange(panel_cols, dtype=jnp.int32)[:, None], prior_weight[None, :half], 0.0
    )
    n_obs_dev = lax.axis_size("obs")
    me = lax.axis_index("obs")
    rows = bw // n_obs_dev
    my_block = jnp.sum(jnp.where(block_owner == my_j, block_range, 0))
    col_index = jnp.arange(panel_cols, dtype=jnp.int32)

    pieces = owned.reshape(n_obs_dev, rows, panel_cols)
    got = [pieces[me]] + [
        lax.ppermute(pieces[(me + s) % n_obs_dev], "obs", [(i, (i + s) % n_obs_dev) for i in range(n_obs_dev)])
        for s in range(1, n_obs_dev)
    ]
    ordered = jnp.stack(got)
    parts = [ordered[(me - src) % n_obs_dev] for src in range(n_obs_dev)]
    while len(parts) > 1:
        parts = [parts[i] + parts[i + 1] for i in range(0, len(parts), 2)]
    slab = parts[0]
    row_index = my_block * bw + me * rows + jnp.arange(rows, dtype=jnp.int32)
    slab = slab + jnp.where(col_index[None, :] == row_index[:, None], prior_weight[None, :], 0.0)

    inverse = factor_inverse(0.5 * (square[:half] + square[:half].T))
    coupling = jnp.dot(square[half:], inverse.T, precision=HI, preferred_element_type=jnp.float32)
    first_slab = jnp.dot(slab[:, :half], inverse.T, precision=HI, preferred_element_type=jnp.float32)
    update_slab = slab[:, half:] - jnp.dot(
        first_slab, coupling.T, precision=HI, preferred_element_type=jnp.float32
    )
    done = jnp.concatenate([first_slab, update_slab], axis=1)
    spread = [done] + [
        lax.ppermute(done, "obs", [(i, (i + s) % n_obs_dev) for i in range(n_obs_dev)])
        for s in range(1, n_obs_dev)
    ]
    ordered = jnp.stack(spread)
    full = jnp.concatenate([ordered[(me - src) % n_obs_dev] for src in range(n_obs_dev)], axis=0)
    first_rows = full[:, :half]
    update_rows = full[:, half:]
    return (first_rows, update_rows)


def solution(mesh):
    in_specs = (P(("obs", "blk"), None, None), P(("obs", "blk"), None), P(("obs", "blk")), P(), P())
    out_specs = (P("blk", None), P("blk", None))
    return jax.shard_map(local, mesh=mesh, in_specs=in_specs, out_specs=out_specs, check_vma=False)
```

```python
import jax
import jax.numpy as jnp
from jax import lax
from jax.sharding import PartitionSpec as P

CAP = 24
HI = lax.Precision.HIGHEST
FIRST = 8


def dot(a, b):
    return jnp.dot(a, b, precision=HI, preferred_element_type=jnp.float32)


def factor_inverse(mirrored):
    n = mirrored.shape[0] // 2
    eye = jnp.eye(n, dtype=jnp.float32)
    low = jnp.linalg.cholesky(mirrored[:n, :n])
    low_inv = jax.scipy.linalg.solve_triangular(low, eye, lower=True)
    left = dot(mirrored[n:, :n], low_inv.T)
    high = jnp.linalg.cholesky(mirrored[n:, n:] - dot(left, left.T))
    high_inv = jax.scipy.linalg.solve_triangular(high, eye, lower=True)
    corner = -dot(high_inv, dot(left, low_inv))
    return jnp.concatenate(
        [jnp.concatenate([low_inv, jnp.zeros_like(low_inv)], axis=1), jnp.concatenate([corner, high_inv], axis=1)],
        axis=0,
    )


def select_columns(labels, design_tiles, wanted):
    touched = design_tiles.shape[1]
    columns = jnp.zeros(
        (design_tiles.shape[0], wanted.shape[0], design_tiles.shape[2]), jnp.float32
    )
    for entry in range(touched):
        hit = labels[:, entry, None] == wanted[None, :]
        columns = columns + jnp.where(hit[:, :, None], design_tiles[:, entry, None, :], 0.0)
    return columns.reshape(design_tiles.shape[0], wanted.shape[0] * design_tiles.shape[2])


def obs_butterfly(x):
    n = lax.axis_size("obs")
    step = 1
    while step < n:
        perm = [(i, i ^ step) for i in range(n)]
        x = x + lax.ppermute(x, "obs", perm)
        step *= 2
    return x


def ranked(labels, wanted):
    hit = jnp.sum((labels[:, :, None] == wanted[None, None, :]).astype(jnp.int32), axis=1)
    cum = jnp.cumsum(hit, axis=0)
    rank_range = jnp.arange(CAP, dtype=jnp.int32)
    sel = jnp.sum((cum[:, :, None] <= rank_range[None, None, :]).astype(jnp.int32), axis=0)
    valid = rank_range[None, :] < cum[-1][:, None]
    return jnp.minimum(sel, labels.shape[0] - 1), valid


def local(design_tiles, block_ids, obs_weight, block_owner, prior_weight):
    n_obs, touched, bw = design_tiles.shape
    nblk = block_owner.shape[0]
    panel_cols = prior_weight.shape[0]
    half = panel_cols // 2
    panel_blocks = panel_cols // bw
    nb = lax.axis_size("blk")
    my_j = lax.axis_index("blk")
    block_range = jnp.arange(nblk, dtype=jnp.int32)
    dest_range = jnp.arange(nb, dtype=jnp.int32)

    inv_owner = jnp.sum(
        jnp.where(block_owner[None, :] == dest_range[:, None], block_range[None, :], 0), axis=1
    )
    slot_owner = jnp.sum(
        jnp.where(block_ids[:, :, None] == block_range[None, None, :], block_owner[None, None, :], 0),
        axis=2,
    )
    hit = slot_owner[:, :, None] == dest_range[None, None, :]
    touch = jnp.sum(hit.astype(jnp.int32), axis=1)
    cum = jnp.cumsum(touch, axis=0)
    rank_range = jnp.arange(CAP, dtype=jnp.int32)
    obs_sel = jnp.sum((cum[:, :, None] <= rank_range[None, None, :]).astype(jnp.int32), axis=0)
    valid = rank_range[None, :] < cum[-1][:, None]
    obs_sel = jnp.minimum(obs_sel, n_obs - 1)
    owners_sel = slot_owner[obs_sel]
    k_sel = jnp.sum(
        jnp.where(owners_sel == dest_range[:, None, None], jnp.arange(touched, dtype=jnp.int32), 0),
        axis=2,
    )
    flat_tiles = design_tiles.reshape(n_obs * touched, bw)
    tile_rows = flat_tiles[obs_sel * touched + k_sel]

    panel_design = select_columns(
        block_ids, design_tiles, jnp.arange(panel_blocks, dtype=jnp.int32)
    )
    weighted = panel_design * obs_weight[:, None]
    panel_rows = weighted[obs_sel]
    tile_rows = jnp.where(valid[:, :, None], tile_rows, 0.0)
    panel_rows = jnp.where(valid[:, :, None], panel_rows, 0.0)

    gram = jnp.einsum("op,oq->pq", weighted, panel_design[:, :half], precision=HI)
    gram_rows = panel_cols // nb
    got_gram = lax.all_to_all(gram.reshape(nb, gram_rows, half), "blk", 0, 0, tiled=True)
    gram_part = obs_butterfly(jnp.sum(got_gram, axis=0))
    spread = jnp.broadcast_to(gram_part[None], (nb, gram_rows, half))
    square = lax.all_to_all(spread, "blk", 0, 0, tiled=True).reshape(panel_cols, half)
    diag = jnp.arange(half, dtype=jnp.int32)
    square = square + jnp.where(
        diag[None, :] == jnp.arange(panel_cols, dtype=jnp.int32)[:, None], prior_weight[None, :half], 0.0
    )

    panel_range = jnp.arange(panel_blocks, dtype=jnp.int32)
    panel_sel, panel_valid = ranked(block_ids, panel_range)
    panel_tiles = weighted.reshape(n_obs, panel_blocks, bw)[panel_sel, panel_range[:, None]]
    panel_tiles = jnp.where(panel_valid[:, :, None], panel_tiles, 0.0)
    id_rows = block_ids.astype(jnp.float32).reshape(-1, bw)
    shared = lax.all_gather(
        jnp.concatenate([panel_tiles.reshape(-1, bw), id_rows], axis=0), "blk", axis=0, tiled=False
    )
    got_tiles = lax.all_to_all(tile_rows, "blk", 0, 0, tiled=True)

    n_panel_rows = panel_blocks * CAP
    src_panel = shared[:, :n_panel_rows].reshape(nb, panel_blocks, CAP, bw)
    src_ids = shared[:, n_panel_rows:].reshape(nb, n_obs, touched).astype(jnp.int32)
    my_block = jnp.sum(jnp.where(block_owner == my_j, block_range, 0))
    mine_sel, mine_valid = jax.vmap(lambda ids: ranked(ids, my_block[None]))(src_ids)
    src_sel, src_valid = jax.vmap(lambda ids: ranked(ids, panel_range))(src_ids)
    match = (
        (mine_sel[:, 0, :, None, None] == src_sel[:, None, :, :])
        & mine_valid[:, 0, :, None, None]
        & src_valid[:, None, :, :]
    ).astype(jnp.float32)
    slot_panel = jnp.einsum("srpq,spqc->srpc", match, src_panel, precision=HI)
    owned = jnp.einsum(
        "si,sp->ip", got_tiles.reshape(nb * CAP, bw), slot_panel.reshape(nb * CAP, panel_cols), precision=HI
    )

    n_obs_dev = lax.axis_size("obs")
    me = lax.axis_index("obs")
    rows = bw // n_obs_dev
    col_index = jnp.arange(panel_cols, dtype=jnp.int32)

    pieces = owned.reshape(n_obs_dev, rows, panel_cols)
    got = [pieces[me]] + [
        lax.ppermute(pieces[(me + s) % n_obs_dev], "obs", [(i, (i + s) % n_obs_dev) for i in range(n_obs_dev)])
        for s in range(1, n_obs_dev)
    ]
    ordered = jnp.stack(got)
    parts = [ordered[(me - src) % n_obs_dev] for src in range(n_obs_dev)]
    while len(parts) > 1:
        parts = [parts[i] + parts[i + 1] for i in range(0, len(parts), 2)]
    slab = parts[0]
    row_index = my_block * bw + me * rows + jnp.arange(rows, dtype=jnp.int32)
    slab = slab + jnp.where(col_index[None, :] == row_index[:, None], prior_weight[None, :], 0.0)

    inverse = factor_inverse(0.5 * (square[:half] + square[:half].T))
    coupling = jnp.dot(square[half:], inverse.T, precision=HI, preferred_element_type=jnp.float32)
    first_slab = jnp.dot(slab[:, :half], inverse.T, precision=HI, preferred_element_type=jnp.float32)
    update_slab = slab[:, half:] - jnp.dot(
        first_slab, coupling.T, precision=HI, preferred_element_type=jnp.float32
    )
    done = jnp.concatenate([first_slab, update_slab], axis=1)
    spread = [done] + [
        lax.ppermute(done, "obs", [(i, (i + s) % n_obs_dev) for i in range(n_obs_dev)])
        for s in range(1, n_obs_dev)
    ]
    ordered = jnp.stack(spread)
    full = jnp.concatenate([ordered[(me - src) % n_obs_dev] for src in range(n_obs_dev)], axis=0)
    first_rows = full[:, :half]
    update_rows = full[:, half:]
    return (first_rows, update_rows)


def solution(mesh):
    in_specs = (P(("obs", "blk"), None, None), P(("obs", "blk"), None), P(("obs", "blk")), P(), P())
    out_specs = (P("blk", None), P("blk", None))
    return jax.shard_map(local, mesh=mesh, in_specs=in_specs, out_specs=out_specs, check_vma=False)
```

```python
import jax
import jax.numpy as jnp
from jax import lax
from jax.sharding import PartitionSpec as P

CAP = 24
HI = lax.Precision.HIGHEST
FIRST = 8


def dot(a, b):
    return jnp.dot(a, b, precision=HI, preferred_element_type=jnp.float32)


def factor_inverse(mirrored):
    n = mirrored.shape[0] // 2
    eye = jnp.eye(n, dtype=jnp.float32)
    low = jnp.linalg.cholesky(mirrored[:n, :n])
    low_inv = jax.scipy.linalg.solve_triangular(low, eye, lower=True)
    left = dot(mirrored[n:, :n], low_inv.T)
    high = jnp.linalg.cholesky(mirrored[n:, n:] - dot(left, left.T))
    high_inv = jax.scipy.linalg.solve_triangular(high, eye, lower=True)
    corner = -dot(high_inv, dot(left, low_inv))
    return jnp.concatenate(
        [jnp.concatenate([low_inv, jnp.zeros_like(low_inv)], axis=1), jnp.concatenate([corner, high_inv], axis=1)],
        axis=0,
    )


def select_columns(labels, design_tiles, wanted):
    touched = design_tiles.shape[1]
    columns = jnp.zeros(
        (design_tiles.shape[0], wanted.shape[0], design_tiles.shape[2]), jnp.float32
    )
    for entry in range(touched):
        hit = labels[:, entry, None] == wanted[None, :]
        columns = columns + jnp.where(hit[:, :, None], design_tiles[:, entry, None, :], 0.0)
    return columns.reshape(design_tiles.shape[0], wanted.shape[0] * design_tiles.shape[2])


def obs_butterfly(x):
    n = lax.axis_size("obs")
    step = 1
    while step < n:
        perm = [(i, i ^ step) for i in range(n)]
        x = x + lax.ppermute(x, "obs", perm)
        step *= 2
    return x


def ranked(labels, wanted):
    hit = jnp.sum((labels[:, :, None] == wanted[None, None, :]).astype(jnp.int32), axis=1)
    cum = jnp.cumsum(hit, axis=0)
    rank_range = jnp.arange(CAP, dtype=jnp.int32)
    sel = jnp.sum((cum[:, :, None] <= rank_range[None, None, :]).astype(jnp.int32), axis=0)
    valid = rank_range[None, :] < cum[-1][:, None]
    return jnp.minimum(sel, labels.shape[0] - 1), valid


def local(design_tiles, block_ids, obs_weight, block_owner, prior_weight):
    n_obs, touched, bw = design_tiles.shape
    nblk = block_owner.shape[0]
    panel_cols = prior_weight.shape[0]
    half = panel_cols // 2
    panel_blocks = panel_cols // bw
    nb = lax.axis_size("blk")
    my_j = lax.axis_index("blk")
    block_range = jnp.arange(nblk, dtype=jnp.int32)
    dest_range = jnp.arange(nb, dtype=jnp.int32)

    inv_owner = jnp.sum(
        jnp.where(block_owner[None, :] == dest_range[:, None], block_range[None, :], 0), axis=1
    )
    slot_owner = jnp.sum(
        jnp.where(block_ids[:, :, None] == block_range[None, None, :], block_owner[None, None, :], 0),
        axis=2,
    )
    hit = slot_owner[:, :, None] == dest_range[None, None, :]
    touch = jnp.sum(hit.astype(jnp.int32), axis=1)
    cum = jnp.cumsum(touch, axis=0)
    rank_range = jnp.arange(CAP, dtype=jnp.int32)
    obs_sel = jnp.sum((cum[:, :, None] <= rank_range[None, None, :]).astype(jnp.int32), axis=0)
    valid = rank_range[None, :] < cum[-1][:, None]
    obs_sel = jnp.minimum(obs_sel, n_obs - 1)
    owners_sel = slot_owner[obs_sel]
    k_sel = jnp.sum(
        jnp.where(owners_sel == dest_range[:, None, None], jnp.arange(touched, dtype=jnp.int32), 0),
        axis=2,
    )
    flat_tiles = design_tiles.reshape(n_obs * touched, bw)
    tile_rows = flat_tiles[obs_sel * touched + k_sel]

    panel_design = select_columns(
        block_ids, design_tiles, jnp.arange(panel_blocks, dtype=jnp.int32)
    )
    weighted = panel_design * obs_weight[:, None]
    panel_rows = weighted[obs_sel]
    tile_rows = jnp.where(valid[:, :, None], tile_rows, 0.0)
    panel_rows = jnp.where(valid[:, :, None], panel_rows, 0.0)

    gram = jnp.einsum("op,oq->pq", weighted, panel_design[:, :half], precision=HI)
    gram_rows = panel_cols // nb
    got_gram = lax.all_to_all(gram.reshape(nb, gram_rows, half), "blk", 0, 0, tiled=True)
    gram_part = obs_butterfly(jnp.sum(got_gram, axis=0))
    spread = jnp.broadcast_to(gram_part[None], (nb, gram_rows, half))

    panel_range = jnp.arange(panel_blocks, dtype=jnp.int32)
    panel_sel, panel_valid = ranked(block_ids, panel_range)
    panel_tiles = weighted.reshape(n_obs, panel_blocks, bw)[panel_sel, panel_range[:, None]]
    panel_tiles = jnp.where(panel_valid[:, :, None], panel_tiles, 0.0)
    shared = lax.all_gather(panel_tiles.reshape(-1, bw), "blk", axis=0, tiled=False)

    panel_hit = jnp.sum((block_ids[:, :, None] == panel_range[None, None, :]).astype(jnp.int32), axis=1)
    panel_pos = jnp.where(panel_hit > 0, jnp.cumsum(panel_hit, axis=0) - 1, CAP)
    slot_pos = jnp.where(valid[:, :, None], panel_pos[obs_sel], CAP).astype(jnp.float32)
    index_width = CAP * panel_blocks // gram_rows
    payload = jnp.concatenate(
        [
            spread,
            tile_rows.reshape(nb, gram_rows, -1),
            slot_pos.reshape(nb, gram_rows, index_width),
        ],
        axis=2,
    )
    got = lax.all_to_all(payload, "blk", 0, 0, tiled=True)
    square = got[:, :, :half].reshape(panel_cols, half)
    got_tiles = got[:, :, half : half + CAP * bw // gram_rows].reshape(nb * CAP, bw)
    got_pos = got[:, :, half + CAP * bw // gram_rows :].reshape(nb, CAP, panel_blocks).astype(jnp.int32)
    diag = jnp.arange(half, dtype=jnp.int32)
    square = square + jnp.where(
        diag[None, :] == jnp.arange(panel_cols, dtype=jnp.int32)[:, None], prior_weight[None, :half], 0.0
    )

    src_panel = shared.reshape(nb, panel_blocks, CAP, bw)
    match = (got_pos[:, :, :, None] == jnp.arange(CAP, dtype=jnp.int32)[None, None, None, :]).astype(jnp.float32)
    slot_panel = jnp.einsum("srpq,spqc->srpc", match, src_panel, precision=HI)
    owned = jnp.einsum("si,sp->ip", got_tiles, slot_panel.reshape(nb * CAP, panel_cols), precision=HI)
    my_block = jnp.sum(jnp.where(block_owner == my_j, block_range, 0))

    n_obs_dev = lax.axis_size("obs")
    me = lax.axis_index("obs")
    rows = bw // n_obs_dev
    col_index = jnp.arange(panel_cols, dtype=jnp.int32)

    pieces = owned.reshape(n_obs_dev, rows, panel_cols)
    got = [pieces[me]] + [
        lax.ppermute(pieces[(me + s) % n_obs_dev], "obs", [(i, (i + s) % n_obs_dev) for i in range(n_obs_dev)])
        for s in range(1, n_obs_dev)
    ]
    ordered = jnp.stack(got)
    parts = [ordered[(me - src) % n_obs_dev] for src in range(n_obs_dev)]
    while len(parts) > 1:
        parts = [parts[i] + parts[i + 1] for i in range(0, len(parts), 2)]
    slab = parts[0]
    row_index = my_block * bw + me * rows + jnp.arange(rows, dtype=jnp.int32)
    slab = slab + jnp.where(col_index[None, :] == row_index[:, None], prior_weight[None, :], 0.0)

    inverse = factor_inverse(0.5 * (square[:half] + square[:half].T))
    coupling = jnp.dot(square[half:], inverse.T, precision=HI, preferred_element_type=jnp.float32)
    first_slab = jnp.dot(slab[:, :half], inverse.T, precision=HI, preferred_element_type=jnp.float32)
    update_slab = slab[:, half:] - jnp.dot(
        first_slab, coupling.T, precision=HI, preferred_element_type=jnp.float32
    )
    done = jnp.concatenate([first_slab, update_slab], axis=1)
    spread = [done] + [
        lax.ppermute(done, "obs", [(i, (i + s) % n_obs_dev) for i in range(n_obs_dev)])
        for s in range(1, n_obs_dev)
    ]
    ordered = jnp.stack(spread)
    full = jnp.concatenate([ordered[(me - src) % n_obs_dev] for src in range(n_obs_dev)], axis=0)
    first_rows = full[:, :half]
    update_rows = full[:, half:]
    return (first_rows, update_rows)


def solution(mesh):
    in_specs = (P(("obs", "blk"), None, None), P(("obs", "blk"), None), P(("obs", "blk")), P(), P())
    out_specs = (P("blk", None), P("blk", None))
    return jax.shard_map(local, mesh=mesh, in_specs=in_specs, out_specs=out_specs, check_vma=False)
```

```python
import jax
import jax.numpy as jnp
from jax import lax
from jax.sharding import PartitionSpec as P

CAP = 24
HI = lax.Precision.HIGHEST
FIRST = 8


def dot(a, b):
    return jnp.dot(a, b, precision=HI, preferred_element_type=jnp.float32)


def factor_inverse(mirrored):
    n = mirrored.shape[0] // 2
    eye = jnp.eye(n, dtype=jnp.float32)
    low = jnp.linalg.cholesky(mirrored[:n, :n])
    low_inv = jax.scipy.linalg.solve_triangular(low, eye, lower=True)
    left = dot(mirrored[n:, :n], low_inv.T)
    high = jnp.linalg.cholesky(mirrored[n:, n:] - dot(left, left.T))
    high_inv = jax.scipy.linalg.solve_triangular(high, eye, lower=True)
    corner = -dot(high_inv, dot(left, low_inv))
    return jnp.concatenate(
        [jnp.concatenate([low_inv, jnp.zeros_like(low_inv)], axis=1), jnp.concatenate([corner, high_inv], axis=1)],
        axis=0,
    )


def select_columns(labels, design_tiles, wanted):
    touched = design_tiles.shape[1]
    columns = jnp.zeros(
        (design_tiles.shape[0], wanted.shape[0], design_tiles.shape[2]), jnp.float32
    )
    for entry in range(touched):
        hit = labels[:, entry, None] == wanted[None, :]
        columns = columns + jnp.where(hit[:, :, None], design_tiles[:, entry, None, :], 0.0)
    return columns.reshape(design_tiles.shape[0], wanted.shape[0] * design_tiles.shape[2])


def obs_butterfly(x):
    n = lax.axis_size("obs")
    step = 1
    while step < n:
        perm = [(i, i ^ step) for i in range(n)]
        x = x + lax.ppermute(x, "obs", perm)
        step *= 2
    return x


def ranked(labels, wanted):
    hit = jnp.sum((labels[:, :, None] == wanted[None, None, :]).astype(jnp.int32), axis=1)
    cum = jnp.cumsum(hit, axis=0)
    rank_range = jnp.arange(CAP, dtype=jnp.int32)
    sel = jnp.sum((cum[:, :, None] <= rank_range[None, None, :]).astype(jnp.int32), axis=0)
    valid = rank_range[None, :] < cum[-1][:, None]
    return jnp.minimum(sel, labels.shape[0] - 1), valid


def local(design_tiles, block_ids, obs_weight, block_owner, prior_weight):
    n_obs, touched, bw = design_tiles.shape
    nblk = block_owner.shape[0]
    panel_cols = prior_weight.shape[0]
    half = panel_cols // 2
    panel_blocks = panel_cols // bw
    nb = lax.axis_size("blk")
    my_j = lax.axis_index("blk")
    block_range = jnp.arange(nblk, dtype=jnp.int32)
    dest_range = jnp.arange(nb, dtype=jnp.int32)

    inv_owner = jnp.sum(
        jnp.where(block_owner[None, :] == dest_range[:, None], block_range[None, :], 0), axis=1
    )
    slot_owner = jnp.sum(
        jnp.where(block_ids[:, :, None] == block_range[None, None, :], block_owner[None, None, :], 0),
        axis=2,
    )
    hit = slot_owner[:, :, None] == dest_range[None, None, :]
    touch = jnp.sum(hit.astype(jnp.int32), axis=1)
    cum = jnp.cumsum(touch, axis=0)
    rank_range = jnp.arange(CAP, dtype=jnp.int32)
    obs_sel = jnp.sum((cum[:, :, None] <= rank_range[None, None, :]).astype(jnp.int32), axis=0)
    valid = rank_range[None, :] < cum[-1][:, None]
    obs_sel = jnp.minimum(obs_sel, n_obs - 1)
    owners_sel = slot_owner[obs_sel]
    k_sel = jnp.sum(
        jnp.where(owners_sel == dest_range[:, None, None], jnp.arange(touched, dtype=jnp.int32), 0),
        axis=2,
    )
    flat_tiles = design_tiles.reshape(n_obs * touched, bw)
    tile_rows = flat_tiles[obs_sel * touched + k_sel]

    panel_design = select_columns(
        block_ids, design_tiles, jnp.arange(panel_blocks, dtype=jnp.int32)
    )
    weighted = panel_design * obs_weight[:, None]
    panel_rows = weighted[obs_sel]
    tile_rows = jnp.where(valid[:, :, None], tile_rows, 0.0)
    panel_rows = jnp.where(valid[:, :, None], panel_rows, 0.0)

    gram = jnp.einsum("op,oq->pq", weighted, panel_design[:, :half], precision=HI)
    gram_rows = panel_cols // nb
    got_gram = lax.all_to_all(gram.reshape(nb, gram_rows, half), "blk", 0, 0, tiled=True)
    gram_part = obs_butterfly(jnp.sum(got_gram, axis=0))
    spread = jnp.broadcast_to(gram_part[None], (nb, gram_rows, half))

    panel_range = jnp.arange(panel_blocks, dtype=jnp.int32)
    panel_sel, panel_valid = ranked(block_ids, panel_range)
    panel_tiles = weighted.reshape(n_obs, panel_blocks, bw)[panel_sel, panel_range[:, None]]
    panel_tiles = jnp.where(panel_valid[:, :, None], panel_tiles, 0.0)
    shared = lax.all_gather(panel_tiles.reshape(-1, bw), "blk", axis=0, tiled=False)

    panel_hit = jnp.sum((block_ids[:, :, None] == panel_range[None, None, :]).astype(jnp.int32), axis=1)
    panel_pos = jnp.where(panel_hit > 0, jnp.cumsum(panel_hit, axis=0) - 1, CAP)
    slot_pos = jnp.where(valid[:, :, None], panel_pos[obs_sel], CAP).astype(jnp.float32)
    index_width = CAP * panel_blocks // gram_rows
    square = lax.all_to_all(spread, "blk", 0, 0, tiled=True).reshape(panel_cols, half)
    payload = jnp.concatenate(
        [tile_rows.reshape(nb, gram_rows, -1), slot_pos.reshape(nb, gram_rows, index_width)], axis=2
    )
    square, payload = lax.optimization_barrier((square, payload))
    got = lax.all_to_all(payload, "blk", 0, 0, tiled=True)
    got_tiles = got[:, :, : CAP * bw // gram_rows].reshape(nb * CAP, bw)
    got_pos = got[:, :, CAP * bw // gram_rows :].reshape(nb, CAP, panel_blocks).astype(jnp.int32)
    diag = jnp.arange(half, dtype=jnp.int32)
    square = square + jnp.where(
        diag[None, :] == jnp.arange(panel_cols, dtype=jnp.int32)[:, None], prior_weight[None, :half], 0.0
    )

    src_panel = shared.reshape(nb, panel_blocks, CAP, bw)
    match = (got_pos[:, :, :, None] == jnp.arange(CAP, dtype=jnp.int32)[None, None, None, :]).astype(jnp.float32)
    slot_panel = jnp.einsum("srpq,spqc->srpc", match, src_panel, precision=HI)
    owned = jnp.einsum("si,sp->ip", got_tiles, slot_panel.reshape(nb * CAP, panel_cols), precision=HI)
    my_block = jnp.sum(jnp.where(block_owner == my_j, block_range, 0))

    n_obs_dev = lax.axis_size("obs")
    me = lax.axis_index("obs")
    rows = bw // n_obs_dev
    col_index = jnp.arange(panel_cols, dtype=jnp.int32)

    pieces = owned.reshape(n_obs_dev, rows, panel_cols)
    got = [pieces[me]] + [
        lax.ppermute(pieces[(me + s) % n_obs_dev], "obs", [(i, (i + s) % n_obs_dev) for i in range(n_obs_dev)])
        for s in range(1, n_obs_dev)
    ]
    ordered = jnp.stack(got)
    parts = [ordered[(me - src) % n_obs_dev] for src in range(n_obs_dev)]
    while len(parts) > 1:
        parts = [parts[i] + parts[i + 1] for i in range(0, len(parts), 2)]
    slab = parts[0]
    row_index = my_block * bw + me * rows + jnp.arange(rows, dtype=jnp.int32)
    slab = slab + jnp.where(col_index[None, :] == row_index[:, None], prior_weight[None, :], 0.0)

    inverse = factor_inverse(0.5 * (square[:half] + square[:half].T))
    coupling = jnp.dot(square[half:], inverse.T, precision=HI, preferred_element_type=jnp.float32)
    first_slab = jnp.dot(slab[:, :half], inverse.T, precision=HI, preferred_element_type=jnp.float32)
    update_slab = slab[:, half:] - jnp.dot(
        first_slab, coupling.T, precision=HI, preferred_element_type=jnp.float32
    )
    done = jnp.concatenate([first_slab, update_slab], axis=1)
    spread = [done] + [
        lax.ppermute(done, "obs", [(i, (i + s) % n_obs_dev) for i in range(n_obs_dev)])
        for s in range(1, n_obs_dev)
    ]
    ordered = jnp.stack(spread)
    full = jnp.concatenate([ordered[(me - src) % n_obs_dev] for src in range(n_obs_dev)], axis=0)
    first_rows = full[:, :half]
    update_rows = full[:, half:]
    return (first_rows, update_rows)


def solution(mesh):
    in_specs = (P(("obs", "blk"), None, None), P(("obs", "blk"), None), P(("obs", "blk")), P(), P())
    out_specs = (P("blk", None), P("blk", None))
    return jax.shard_map(local, mesh=mesh, in_specs=in_specs, out_specs=out_specs, check_vma=False)
```

```python
import jax
import jax.numpy as jnp
from jax import lax
from jax.sharding import PartitionSpec as P

CAP = 24
HI = lax.Precision.HIGHEST
FIRST = 8


def dot(a, b):
    return jnp.dot(a, b, precision=HI, preferred_element_type=jnp.float32)


def factor_inverse(mirrored):
    n = mirrored.shape[0] // 2
    eye = jnp.eye(n, dtype=jnp.float32)
    low = jnp.linalg.cholesky(mirrored[:n, :n])
    low_inv = jax.scipy.linalg.solve_triangular(low, eye, lower=True)
    left = dot(mirrored[n:, :n], low_inv.T)
    high = jnp.linalg.cholesky(mirrored[n:, n:] - dot(left, left.T))
    high_inv = jax.scipy.linalg.solve_triangular(high, eye, lower=True)
    corner = -dot(high_inv, dot(left, low_inv))
    return jnp.concatenate(
        [jnp.concatenate([low_inv, jnp.zeros_like(low_inv)], axis=1), jnp.concatenate([corner, high_inv], axis=1)],
        axis=0,
    )


def select_columns(labels, design_tiles, wanted):
    touched = design_tiles.shape[1]
    columns = jnp.zeros(
        (design_tiles.shape[0], wanted.shape[0], design_tiles.shape[2]), jnp.float32
    )
    for entry in range(touched):
        hit = labels[:, entry, None] == wanted[None, :]
        columns = columns + jnp.where(hit[:, :, None], design_tiles[:, entry, None, :], 0.0)
    return columns.reshape(design_tiles.shape[0], wanted.shape[0] * design_tiles.shape[2])


def obs_butterfly(x):
    n = lax.axis_size("obs")
    step = 1
    while step < n:
        perm = [(i, i ^ step) for i in range(n)]
        x = x + lax.ppermute(x, "obs", perm)
        step *= 2
    return x


def ranked(labels, wanted):
    hit = jnp.sum((labels[:, :, None] == wanted[None, None, :]).astype(jnp.int32), axis=1)
    cum = jnp.cumsum(hit, axis=0)
    rank_range = jnp.arange(CAP, dtype=jnp.int32)
    sel = jnp.sum((cum[:, :, None] <= rank_range[None, None, :]).astype(jnp.int32), axis=0)
    valid = rank_range[None, :] < cum[-1][:, None]
    return jnp.minimum(sel, labels.shape[0] - 1), valid, jnp.where(hit > 0, cum - 1, CAP)


def local(design_tiles, block_ids, obs_weight, block_owner, prior_weight):
    n_obs, touched, bw = design_tiles.shape
    nblk = block_owner.shape[0]
    panel_cols = prior_weight.shape[0]
    half = panel_cols // 2
    panel_blocks = panel_cols // bw
    nb = lax.axis_size("blk")
    my_j = lax.axis_index("blk")
    block_range = jnp.arange(nblk, dtype=jnp.int32)
    dest_range = jnp.arange(nb, dtype=jnp.int32)

    inv_owner = jnp.sum(
        jnp.where(block_owner[None, :] == dest_range[:, None], block_range[None, :], 0), axis=1
    )
    slot_owner = jnp.sum(
        jnp.where(block_ids[:, :, None] == block_range[None, None, :], block_owner[None, None, :], 0),
        axis=2,
    )
    hit = slot_owner[:, :, None] == dest_range[None, None, :]
    touch = jnp.sum(hit.astype(jnp.int32), axis=1)
    cum = jnp.cumsum(touch, axis=0)
    rank_range = jnp.arange(CAP, dtype=jnp.int32)
    obs_sel = jnp.sum((cum[:, :, None] <= rank_range[None, None, :]).astype(jnp.int32), axis=0)
    valid = rank_range[None, :] < cum[-1][:, None]
    obs_sel = jnp.minimum(obs_sel, n_obs - 1)
    owners_sel = slot_owner[obs_sel]
    k_sel = jnp.sum(
        jnp.where(owners_sel == dest_range[:, None, None], jnp.arange(touched, dtype=jnp.int32), 0),
        axis=2,
    )
    flat_tiles = design_tiles.reshape(n_obs * touched, bw)
    tile_rows = flat_tiles[obs_sel * touched + k_sel]

    panel_design = select_columns(
        block_ids, design_tiles, jnp.arange(panel_blocks, dtype=jnp.int32)
    )
    weighted = panel_design * obs_weight[:, None]
    panel_rows = weighted[obs_sel]
    tile_rows = jnp.where(valid[:, :, None], tile_rows, 0.0)
    panel_rows = jnp.where(valid[:, :, None], panel_rows, 0.0)

    gram = jnp.einsum("op,oq->pq", weighted, panel_design[:, :half], precision=HI)
    gram_rows = panel_cols // nb
    got_gram = lax.all_to_all(gram.reshape(nb, gram_rows, half), "blk", 0, 0, tiled=True)
    gram_part = obs_butterfly(jnp.sum(got_gram, axis=0))
    spread = jnp.broadcast_to(gram_part[None], (nb, gram_rows, half))

    panel_range = jnp.arange(panel_blocks, dtype=jnp.int32)
    panel_sel, panel_valid, panel_pos = ranked(block_ids, panel_range)
    panel_tiles = weighted.reshape(n_obs, panel_blocks, bw)[panel_sel, panel_range[:, None]]
    panel_tiles = jnp.where(panel_valid[:, :, None], panel_tiles, 0.0)
    shared = lax.all_gather(panel_tiles.reshape(-1, bw), "blk", axis=0, tiled=False)

    slot_pos = jnp.where(valid[:, :, None], panel_pos[obs_sel], CAP).astype(jnp.float32)
    index_width = CAP * panel_blocks // gram_rows
    square = lax.all_to_all(spread, "blk", 0, 0, tiled=True).reshape(panel_cols, half)
    payload = jnp.concatenate(
        [tile_rows.reshape(nb, gram_rows, -1), slot_pos.reshape(nb, gram_rows, index_width)], axis=2
    )
    square, payload = lax.optimization_barrier((square, payload))
    got = lax.all_to_all(payload, "blk", 0, 0, tiled=True)
    got_tiles = got[:, :, : CAP * bw // gram_rows].reshape(nb * CAP, bw)
    got_pos = got[:, :, CAP * bw // gram_rows :].reshape(nb, CAP, panel_blocks).astype(jnp.int32)
    diag = jnp.arange(half, dtype=jnp.int32)
    square = square + jnp.where(
        diag[None, :] == jnp.arange(panel_cols, dtype=jnp.int32)[:, None], prior_weight[None, :half], 0.0
    )

    src_panel = jnp.concatenate(
        [shared.reshape(nb, panel_blocks, CAP, bw), jnp.zeros((nb, panel_blocks, 1, bw), jnp.float32)], axis=2
    ).reshape(nb * panel_blocks * (CAP + 1), bw)
    row_of = (
        jnp.arange(nb, dtype=jnp.int32)[:, None, None] * panel_blocks + panel_range[None, None, :]
    ) * (CAP + 1) + got_pos
    slot_panel = src_panel[row_of]
    owned = jnp.einsum("si,sp->ip", got_tiles, slot_panel.reshape(nb * CAP, panel_cols), precision=HI)
    my_block = jnp.sum(jnp.where(block_owner == my_j, block_range, 0))

    owned = obs_butterfly(owned)
    row_index = my_block * bw + jnp.arange(bw, dtype=jnp.int32)
    col_index = jnp.arange(panel_cols, dtype=jnp.int32)
    owned = owned + jnp.where(col_index[None, :] == row_index[:, None], prior_weight[None, :], 0.0)

    inverse = factor_inverse(0.5 * (square[:half] + square[:half].T))
    coupling = jnp.dot(square[half:], inverse.T, precision=HI, preferred_element_type=jnp.float32)
    first_rows = jnp.dot(owned[:, :half], inverse.T, precision=HI, preferred_element_type=jnp.float32)
    update_rows = owned[:, half:] - jnp.dot(
        first_rows, coupling.T, precision=HI, preferred_element_type=jnp.float32
    )
    return (first_rows, update_rows)


def solution(mesh):
    in_specs = (P(("obs", "blk"), None, None), P(("obs", "blk"), None), P(("obs", "blk")), P(), P())
    out_specs = (P("blk", None), P("blk", None))
    return jax.shard_map(local, mesh=mesh, in_specs=in_specs, out_specs=out_specs, check_vma=False)
```

```python
import jax
import jax.numpy as jnp
from jax import lax
from jax.sharding import PartitionSpec as P

CAP = 24
HI = lax.Precision.HIGHEST
FIRST = 8


def dot(a, b):
    return jnp.dot(a, b, precision=HI, preferred_element_type=jnp.float32)


def factor_inverse(mirrored):
    n = mirrored.shape[0] // 2
    eye = jnp.eye(n, dtype=jnp.float32)
    low = jnp.linalg.cholesky(mirrored[:n, :n])
    low_inv = jax.scipy.linalg.solve_triangular(low, eye, lower=True)
    left = dot(mirrored[n:, :n], low_inv.T)
    high = jnp.linalg.cholesky(mirrored[n:, n:] - dot(left, left.T))
    high_inv = jax.scipy.linalg.solve_triangular(high, eye, lower=True)
    corner = -dot(high_inv, dot(left, low_inv))
    return jnp.concatenate(
        [jnp.concatenate([low_inv, jnp.zeros_like(low_inv)], axis=1), jnp.concatenate([corner, high_inv], axis=1)],
        axis=0,
    )


def select_columns(labels, design_tiles, wanted):
    touched = design_tiles.shape[1]
    columns = jnp.zeros(
        (design_tiles.shape[0], wanted.shape[0], design_tiles.shape[2]), jnp.float32
    )
    for entry in range(touched):
        hit = labels[:, entry, None] == wanted[None, :]
        columns = columns + jnp.where(hit[:, :, None], design_tiles[:, entry, None, :], 0.0)
    return columns.reshape(design_tiles.shape[0], wanted.shape[0] * design_tiles.shape[2])


def obs_butterfly(x):
    n = lax.axis_size("obs")
    step = 1
    while step < n:
        perm = [(i, i ^ step) for i in range(n)]
        x = x + lax.ppermute(x, "obs", perm)
        step *= 2
    return x


def ranked(labels, wanted):
    hit = jnp.sum((labels[:, :, None] == wanted[None, None, :]).astype(jnp.int32), axis=1)
    cum = jnp.cumsum(hit, axis=0)
    rank_range = jnp.arange(CAP, dtype=jnp.int32)
    sel = jnp.sum((cum[:, :, None] <= rank_range[None, None, :]).astype(jnp.int32), axis=0)
    valid = rank_range[None, :] < cum[-1][:, None]
    return jnp.minimum(sel, labels.shape[0] - 1), valid, jnp.where(hit > 0, cum - 1, CAP)


def local(design_tiles, block_ids, obs_weight, block_owner, prior_weight):
    n_obs, touched, bw = design_tiles.shape
    nblk = block_owner.shape[0]
    panel_cols = prior_weight.shape[0]
    half = panel_cols // 2
    panel_blocks = panel_cols // bw
    nb = lax.axis_size("blk")
    my_j = lax.axis_index("blk")
    block_range = jnp.arange(nblk, dtype=jnp.int32)
    dest_range = jnp.arange(nb, dtype=jnp.int32)

    inv_owner = jnp.sum(
        jnp.where(block_owner[None, :] == dest_range[:, None], block_range[None, :], 0), axis=1
    )
    slot_owner = jnp.sum(
        jnp.where(block_ids[:, :, None] == block_range[None, None, :], block_owner[None, None, :], 0),
        axis=2,
    )
    hit = slot_owner[:, :, None] == dest_range[None, None, :]
    touch = jnp.sum(hit.astype(jnp.int32), axis=1)
    cum = jnp.cumsum(touch, axis=0)
    rank_range = jnp.arange(CAP, dtype=jnp.int32)
    obs_sel = jnp.sum((cum[:, :, None] <= rank_range[None, None, :]).astype(jnp.int32), axis=0)
    valid = rank_range[None, :] < cum[-1][:, None]
    obs_sel = jnp.minimum(obs_sel, n_obs - 1)
    owners_sel = slot_owner[obs_sel]
    k_sel = jnp.sum(
        jnp.where(owners_sel == dest_range[:, None, None], jnp.arange(touched, dtype=jnp.int32), 0),
        axis=2,
    )
    flat_tiles = design_tiles.reshape(n_obs * touched, bw)
    tile_rows = flat_tiles[obs_sel * touched + k_sel]

    panel_design = select_columns(
        block_ids, design_tiles, jnp.arange(panel_blocks, dtype=jnp.int32)
    )
    weighted = panel_design * obs_weight[:, None]
    panel_rows = weighted[obs_sel]
    tile_rows = jnp.where(valid[:, :, None], tile_rows, 0.0)
    panel_rows = jnp.where(valid[:, :, None], panel_rows, 0.0)

    gram = jnp.einsum("op,oq->pq", weighted, panel_design[:, :half], precision=HI)
    gram_rows = panel_cols // nb
    got_gram = lax.all_to_all(gram.reshape(nb, gram_rows, half), "blk", 0, 0, tiled=True)
    gram_part = obs_butterfly(jnp.sum(got_gram, axis=0))
    spread = jnp.broadcast_to(gram_part[None], (nb, gram_rows, half))

    panel_range = jnp.arange(panel_blocks, dtype=jnp.int32)
    panel_sel, panel_valid, panel_pos = ranked(block_ids, panel_range)
    panel_tiles = weighted.reshape(n_obs, panel_blocks, bw)[panel_sel, panel_range[:, None]]
    panel_tiles = jnp.where(panel_valid[:, :, None], panel_tiles, 0.0)
    shared = lax.all_gather(panel_tiles.reshape(-1, bw), "blk", axis=0, tiled=False)

    slot_pos = jnp.where(valid[:, :, None], panel_pos[obs_sel], CAP).astype(jnp.float32)
    index_width = CAP * panel_blocks // gram_rows
    square = lax.all_to_all(spread, "blk", 0, 0, tiled=True).reshape(panel_cols, half)
    payload = jnp.concatenate(
        [tile_rows.reshape(nb, gram_rows, -1), slot_pos.reshape(nb, gram_rows, index_width)], axis=2
    )
    square, payload = lax.optimization_barrier((square, payload))
    got = lax.all_to_all(payload, "blk", 0, 0, tiled=True)
    got_tiles = got[:, :, : CAP * bw // gram_rows].reshape(nb * CAP, bw)
    got_pos = got[:, :, CAP * bw // gram_rows :].reshape(nb, CAP, panel_blocks).astype(jnp.int32)
    diag = jnp.arange(half, dtype=jnp.int32)
    square = square + jnp.where(
        diag[None, :] == jnp.arange(panel_cols, dtype=jnp.int32)[:, None], prior_weight[None, :half], 0.0
    )

    src_panel = shared.reshape(nb, panel_blocks, CAP, bw)
    match = (got_pos[:, :, :, None] == jnp.arange(CAP, dtype=jnp.int32)[None, None, None, :]).astype(jnp.float32)
    slot_panel = jnp.einsum("srpq,spqc->srpc", match, src_panel, precision=lax.Precision.HIGH)
    owned = jnp.einsum("si,sp->ip", got_tiles, slot_panel.reshape(nb * CAP, panel_cols), precision=HI)
    my_block = jnp.sum(jnp.where(block_owner == my_j, block_range, 0))

    n_obs_dev = lax.axis_size("obs")
    me = lax.axis_index("obs")
    rows = bw // n_obs_dev
    col_index = jnp.arange(panel_cols, dtype=jnp.int32)

    pieces = owned.reshape(n_obs_dev, rows, panel_cols)
    got = [pieces[me]] + [
        lax.ppermute(pieces[(me + s) % n_obs_dev], "obs", [(i, (i + s) % n_obs_dev) for i in range(n_obs_dev)])
        for s in range(1, n_obs_dev)
    ]
    ordered = jnp.stack(got)
    parts = [ordered[(me - src) % n_obs_dev] for src in range(n_obs_dev)]
    while len(parts) > 1:
        parts = [parts[i] + parts[i + 1] for i in range(0, len(parts), 2)]
    slab = parts[0]
    row_index = my_block * bw + me * rows + jnp.arange(rows, dtype=jnp.int32)
    slab = slab + jnp.where(col_index[None, :] == row_index[:, None], prior_weight[None, :], 0.0)

    inverse = factor_inverse(0.5 * (square[:half] + square[:half].T))
    coupling = jnp.dot(square[half:], inverse.T, precision=HI, preferred_element_type=jnp.float32)
    first_slab = jnp.dot(slab[:, :half], inverse.T, precision=HI, preferred_element_type=jnp.float32)
    update_slab = slab[:, half:] - jnp.dot(
        first_slab, coupling.T, precision=HI, preferred_element_type=jnp.float32
    )
    done = jnp.concatenate([first_slab, update_slab], axis=1)
    spread = [done] + [
        lax.ppermute(done, "obs", [(i, (i + s) % n_obs_dev) for i in range(n_obs_dev)])
        for s in range(1, n_obs_dev)
    ]
    ordered = jnp.stack(spread)
    full = jnp.concatenate([ordered[(me - src) % n_obs_dev] for src in range(n_obs_dev)], axis=0)
    first_rows = full[:, :half]
    update_rows = full[:, half:]
    return (first_rows, update_rows)


def solution(mesh):
    in_specs = (P(("obs", "blk"), None, None), P(("obs", "blk"), None), P(("obs", "blk")), P(), P())
    out_specs = (P("blk", None), P("blk", None))
    return jax.shard_map(local, mesh=mesh, in_specs=in_specs, out_specs=out_specs, check_vma=False)
```

```python
import jax
import jax.numpy as jnp
from jax import lax
from jax.sharding import PartitionSpec as P

CAP = 24
HI = lax.Precision.HIGHEST
FIRST = 8


def dot(a, b):
    return jnp.dot(a, b, precision=HI, preferred_element_type=jnp.float32)


def factor_inverse(mirrored):
    n = mirrored.shape[0] // 2
    eye = jnp.eye(n, dtype=jnp.float32)
    low = jnp.linalg.cholesky(mirrored[:n, :n])
    low_inv = jax.scipy.linalg.solve_triangular(low, eye, lower=True)
    left = dot(mirrored[n:, :n], low_inv.T)
    high = jnp.linalg.cholesky(mirrored[n:, n:] - dot(left, left.T))
    high_inv = jax.scipy.linalg.solve_triangular(high, eye, lower=True)
    corner = -dot(high_inv, dot(left, low_inv))
    return jnp.concatenate(
        [jnp.concatenate([low_inv, jnp.zeros_like(low_inv)], axis=1), jnp.concatenate([corner, high_inv], axis=1)],
        axis=0,
    )


def select_columns(labels, design_tiles, wanted):
    touched = design_tiles.shape[1]
    columns = jnp.zeros(
        (design_tiles.shape[0], wanted.shape[0], design_tiles.shape[2]), jnp.float32
    )
    for entry in range(touched):
        hit = labels[:, entry, None] == wanted[None, :]
        columns = columns + jnp.where(hit[:, :, None], design_tiles[:, entry, None, :], 0.0)
    return columns.reshape(design_tiles.shape[0], wanted.shape[0] * design_tiles.shape[2])


def obs_butterfly(x):
    n = lax.axis_size("obs")
    step = 1
    while step < n:
        perm = [(i, i ^ step) for i in range(n)]
        x = x + lax.ppermute(x, "obs", perm)
        step *= 2
    return x


def ranked(labels, wanted):
    hit = jnp.sum((labels[:, :, None] == wanted[None, None, :]).astype(jnp.int32), axis=1)
    cum = jnp.cumsum(hit, axis=0)
    rank_range = jnp.arange(CAP, dtype=jnp.int32)
    sel = jnp.sum((cum[:, :, None] <= rank_range[None, None, :]).astype(jnp.int32), axis=0)
    valid = rank_range[None, :] < cum[-1][:, None]
    return jnp.minimum(sel, labels.shape[0] - 1), valid


def local(design_tiles, block_ids, obs_weight, block_owner, prior_weight):
    n_obs, touched, bw = design_tiles.shape
    nblk = block_owner.shape[0]
    panel_cols = prior_weight.shape[0]
    half = panel_cols // 2
    panel_blocks = panel_cols // bw
    nb = lax.axis_size("blk")
    my_j = lax.axis_index("blk")
    block_range = jnp.arange(nblk, dtype=jnp.int32)
    dest_range = jnp.arange(nb, dtype=jnp.int32)

    inv_owner = jnp.sum(
        jnp.where(block_owner[None, :] == dest_range[:, None], block_range[None, :], 0), axis=1
    )
    slot_owner = jnp.sum(
        jnp.where(block_ids[:, :, None] == block_range[None, None, :], block_owner[None, None, :], 0),
        axis=2,
    )
    hit = slot_owner[:, :, None] == dest_range[None, None, :]
    touch = jnp.sum(hit.astype(jnp.int32), axis=1)
    cum = jnp.cumsum(touch, axis=0)
    rank_range = jnp.arange(CAP, dtype=jnp.int32)
    obs_sel = jnp.sum((cum[:, :, None] <= rank_range[None, None, :]).astype(jnp.int32), axis=0)
    valid = rank_range[None, :] < cum[-1][:, None]
    obs_sel = jnp.minimum(obs_sel, n_obs - 1)
    owners_sel = slot_owner[obs_sel]
    k_sel = jnp.sum(
        jnp.where(owners_sel == dest_range[:, None, None], jnp.arange(touched, dtype=jnp.int32), 0),
        axis=2,
    )
    flat_tiles = design_tiles.reshape(n_obs * touched, bw)
    tile_rows = flat_tiles[obs_sel * touched + k_sel]

    panel_design = select_columns(
        block_ids, design_tiles, jnp.arange(panel_blocks, dtype=jnp.int32)
    )
    weighted = panel_design * obs_weight[:, None]
    panel_rows = weighted[obs_sel]
    tile_rows = jnp.where(valid[:, :, None], tile_rows, 0.0)
    panel_rows = jnp.where(valid[:, :, None], panel_rows, 0.0)

    gram = jnp.einsum("op,oq->pq", weighted, panel_design[:, :half], precision=HI)
    gram_rows = panel_cols // nb
    got_gram = lax.all_to_all(gram.reshape(nb, gram_rows, half), "blk", 0, 0, tiled=True)
    gram_part = obs_butterfly(jnp.sum(got_gram, axis=0))
    spread = jnp.broadcast_to(gram_part[None], (nb, gram_rows, half))

    panel_range = jnp.arange(panel_blocks, dtype=jnp.int32)
    panel_sel, panel_valid = ranked(block_ids, panel_range)
    panel_tiles = weighted.reshape(n_obs, panel_blocks, bw)[panel_sel, panel_range[:, None]]
    panel_tiles = jnp.where(panel_valid[:, :, None], panel_tiles, 0.0)
    shared = lax.all_gather(panel_tiles.reshape(-1, bw), "blk", axis=0, tiled=False)

    panel_hit = jnp.sum((block_ids[:, :, None] == panel_range[None, None, :]).astype(jnp.int32), axis=1)
    panel_pos = jnp.where(panel_hit > 0, jnp.cumsum(panel_hit, axis=0) - 1, CAP)
    slot_pos = jnp.where(valid[:, :, None], panel_pos[obs_sel], CAP).astype(jnp.float32)
    index_width = CAP * panel_blocks // gram_rows
    square = lax.all_to_all(spread, "blk", 0, 0, tiled=True).reshape(panel_cols, half)
    payload = jnp.concatenate(
        [tile_rows.reshape(nb, gram_rows, -1), slot_pos.reshape(nb, gram_rows, index_width)], axis=2
    )
    square, payload = lax.optimization_barrier((square, payload))
    got = lax.all_to_all(payload, "blk", 0, 0, tiled=True)
    got_tiles = got[:, :, : CAP * bw // gram_rows].reshape(nb * CAP, bw)
    got_pos = got[:, :, CAP * bw // gram_rows :].reshape(nb, CAP, panel_blocks).astype(jnp.int32)
    diag = jnp.arange(half, dtype=jnp.int32)
    square = square + jnp.where(
        diag[None, :] == jnp.arange(panel_cols, dtype=jnp.int32)[:, None], prior_weight[None, :half], 0.0
    )

    src_panel = shared.reshape(nb, panel_blocks, CAP, bw)
    match = (got_pos[:, :, :, None] == jnp.arange(CAP, dtype=jnp.int32)[None, None, None, :]).astype(jnp.float32)
    slot_panel = jnp.einsum("srpq,spqc->srpc", match, src_panel, precision=HI)
    owned = jnp.einsum(
        "sri,srpc->ipc", got_tiles.reshape(nb, CAP, bw), slot_panel, precision=HI
    ).reshape(bw, panel_cols)
    my_block = jnp.sum(jnp.where(block_owner == my_j, block_range, 0))

    n_obs_dev = lax.axis_size("obs")
    me = lax.axis_index("obs")
    rows = bw // n_obs_dev
    col_index = jnp.arange(panel_cols, dtype=jnp.int32)

    pieces = owned.reshape(n_obs_dev, rows, panel_cols)
    got = [pieces[me]] + [
        lax.ppermute(pieces[(me + s) % n_obs_dev], "obs", [(i, (i + s) % n_obs_dev) for i in range(n_obs_dev)])
        for s in range(1, n_obs_dev)
    ]
    ordered = jnp.stack(got)
    parts = [ordered[(me - src) % n_obs_dev] for src in range(n_obs_dev)]
    while len(parts) > 1:
        parts = [parts[i] + parts[i + 1] for i in range(0, len(parts), 2)]
    slab = parts[0]
    row_index = my_block * bw + me * rows + jnp.arange(rows, dtype=jnp.int32)
    slab = slab + jnp.where(col_index[None, :] == row_index[:, None], prior_weight[None, :], 0.0)

    inverse = factor_inverse(0.5 * (square[:half] + square[:half].T))
    coupling = jnp.dot(square[half:], inverse.T, precision=HI, preferred_element_type=jnp.float32)
    first_slab = jnp.dot(slab[:, :half], inverse.T, precision=HI, preferred_element_type=jnp.float32)
    update_slab = slab[:, half:] - jnp.dot(
        first_slab, coupling.T, precision=HI, preferred_element_type=jnp.float32
    )
    done = jnp.concatenate([first_slab, update_slab], axis=1)
    spread = [done] + [
        lax.ppermute(done, "obs", [(i, (i + s) % n_obs_dev) for i in range(n_obs_dev)])
        for s in range(1, n_obs_dev)
    ]
    ordered = jnp.stack(spread)
    full = jnp.concatenate([ordered[(me - src) % n_obs_dev] for src in range(n_obs_dev)], axis=0)
    first_rows = full[:, :half]
    update_rows = full[:, half:]
    return (first_rows, update_rows)


def solution(mesh):
    in_specs = (P(("obs", "blk"), None, None), P(("obs", "blk"), None), P(("obs", "blk")), P(), P())
    out_specs = (P("blk", None), P("blk", None))
    return jax.shard_map(local, mesh=mesh, in_specs=in_specs, out_specs=out_specs, check_vma=False)
```

```python
import jax
import jax.numpy as jnp
from jax import lax
from jax.sharding import PartitionSpec as P

CAP = 24
HI = lax.Precision.HIGHEST
FIRST = 8


def dot(a, b):
    return jnp.dot(a, b, precision=HI, preferred_element_type=jnp.float32)


def factor_inverse(mirrored):
    n = mirrored.shape[0] // 2
    eye = jnp.eye(n, dtype=jnp.float32)
    low = jnp.linalg.cholesky(mirrored[:n, :n])
    low_inv = jax.scipy.linalg.solve_triangular(low, eye, lower=True)
    left = dot(mirrored[n:, :n], low_inv.T)
    high = jnp.linalg.cholesky(mirrored[n:, n:] - dot(left, left.T))
    high_inv = jax.scipy.linalg.solve_triangular(high, eye, lower=True)
    corner = -dot(high_inv, dot(left, low_inv))
    return jnp.concatenate(
        [jnp.concatenate([low_inv, jnp.zeros_like(low_inv)], axis=1), jnp.concatenate([corner, high_inv], axis=1)],
        axis=0,
    )


def select_columns(labels, design_tiles, wanted):
    touched = design_tiles.shape[1]
    columns = jnp.zeros(
        (design_tiles.shape[0], wanted.shape[0], design_tiles.shape[2]), jnp.float32
    )
    for entry in range(touched):
        hit = labels[:, entry, None] == wanted[None, :]
        columns = columns + jnp.where(hit[:, :, None], design_tiles[:, entry, None, :], 0.0)
    return columns.reshape(design_tiles.shape[0], wanted.shape[0] * design_tiles.shape[2])


def obs_butterfly(x):
    n = lax.axis_size("obs")
    me = lax.axis_index("obs")
    got = [x] + [lax.ppermute(x, "obs", [(i, (i + s) % n) for i in range(n)]) for s in range(1, n)]
    ordered = jnp.stack(got)
    parts = [ordered[(me - src) % n] for src in range(n)]
    while len(parts) > 1:
        parts = [parts[i] + parts[i + 1] for i in range(0, len(parts), 2)]
    return parts[0]


def ranked(labels, wanted):
    hit = jnp.sum((labels[:, :, None] == wanted[None, None, :]).astype(jnp.int32), axis=1)
    cum = jnp.cumsum(hit, axis=0)
    rank_range = jnp.arange(CAP, dtype=jnp.int32)
    sel = jnp.sum((cum[:, :, None] <= rank_range[None, None, :]).astype(jnp.int32), axis=0)
    valid = rank_range[None, :] < cum[-1][:, None]
    return jnp.minimum(sel, labels.shape[0] - 1), valid


def local(design_tiles, block_ids, obs_weight, block_owner, prior_weight):
    n_obs, touched, bw = design_tiles.shape
    nblk = block_owner.shape[0]
    panel_cols = prior_weight.shape[0]
    half = panel_cols // 2
    panel_blocks = panel_cols // bw
    nb = lax.axis_size("blk")
    my_j = lax.axis_index("blk")
    block_range = jnp.arange(nblk, dtype=jnp.int32)
    dest_range = jnp.arange(nb, dtype=jnp.int32)

    inv_owner = jnp.sum(
        jnp.where(block_owner[None, :] == dest_range[:, None], block_range[None, :], 0), axis=1
    )
    slot_owner = jnp.sum(
        jnp.where(block_ids[:, :, None] == block_range[None, None, :], block_owner[None, None, :], 0),
        axis=2,
    )
    hit = slot_owner[:, :, None] == dest_range[None, None, :]
    touch = jnp.sum(hit.astype(jnp.int32), axis=1)
    cum = jnp.cumsum(touch, axis=0)
    rank_range = jnp.arange(CAP, dtype=jnp.int32)
    obs_sel = jnp.sum((cum[:, :, None] <= rank_range[None, None, :]).astype(jnp.int32), axis=0)
    valid = rank_range[None, :] < cum[-1][:, None]
    obs_sel = jnp.minimum(obs_sel, n_obs - 1)
    owners_sel = slot_owner[obs_sel]
    k_sel = jnp.sum(
        jnp.where(owners_sel == dest_range[:, None, None], jnp.arange(touched, dtype=jnp.int32), 0),
        axis=2,
    )
    flat_tiles = design_tiles.reshape(n_obs * touched, bw)
    tile_rows = flat_tiles[obs_sel * touched + k_sel]

    panel_design = select_columns(
        block_ids, design_tiles, jnp.arange(panel_blocks, dtype=jnp.int32)
    )
    weighted = panel_design * obs_weight[:, None]
    panel_rows = weighted[obs_sel]
    tile_rows = jnp.where(valid[:, :, None], tile_rows, 0.0)
    panel_rows = jnp.where(valid[:, :, None], panel_rows, 0.0)

    gram = jnp.einsum("op,oq->pq", weighted, panel_design[:, :half], precision=HI)
    gram_rows = panel_cols // nb
    got_gram = lax.all_to_all(gram.reshape(nb, gram_rows, half), "blk", 0, 0, tiled=True)
    gram_part = obs_butterfly(jnp.sum(got_gram, axis=0))
    spread = jnp.broadcast_to(gram_part[None], (nb, gram_rows, half))

    panel_range = jnp.arange(panel_blocks, dtype=jnp.int32)
    panel_sel, panel_valid = ranked(block_ids, panel_range)
    panel_tiles = weighted.reshape(n_obs, panel_blocks, bw)[panel_sel, panel_range[:, None]]
    panel_tiles = jnp.where(panel_valid[:, :, None], panel_tiles, 0.0)
    shared = lax.all_gather(panel_tiles.reshape(-1, bw), "blk", axis=0, tiled=False)

    panel_hit = jnp.sum((block_ids[:, :, None] == panel_range[None, None, :]).astype(jnp.int32), axis=1)
    panel_pos = jnp.where(panel_hit > 0, jnp.cumsum(panel_hit, axis=0) - 1, CAP)
    slot_pos = jnp.where(valid[:, :, None], panel_pos[obs_sel], CAP).astype(jnp.float32)
    index_width = CAP * panel_blocks // gram_rows
    square = lax.all_to_all(spread, "blk", 0, 0, tiled=True).reshape(panel_cols, half)
    payload = jnp.concatenate(
        [tile_rows.reshape(nb, gram_rows, -1), slot_pos.reshape(nb, gram_rows, index_width)], axis=2
    )
    square, payload = lax.optimization_barrier((square, payload))
    got = lax.all_to_all(payload, "blk", 0, 0, tiled=True)
    got_tiles = got[:, :, : CAP * bw // gram_rows].reshape(nb * CAP, bw)
    got_pos = got[:, :, CAP * bw // gram_rows :].reshape(nb, CAP, panel_blocks).astype(jnp.int32)
    diag = jnp.arange(half, dtype=jnp.int32)
    square = square + jnp.where(
        diag[None, :] == jnp.arange(panel_cols, dtype=jnp.int32)[:, None], prior_weight[None, :half], 0.0
    )

    src_panel = shared.reshape(nb, panel_blocks, CAP, bw)
    match = (got_pos[:, :, :, None] == jnp.arange(CAP, dtype=jnp.int32)[None, None, None, :]).astype(jnp.float32)
    slot_panel = jnp.einsum("srpq,spqc->srpc", match, src_panel, precision=HI)
    owned = jnp.einsum(
        "sri,srpc->ipc", got_tiles.reshape(nb, CAP, bw), slot_panel, precision=HI
    ).reshape(bw, panel_cols)
    my_block = jnp.sum(jnp.where(block_owner == my_j, block_range, 0))

    n_obs_dev = lax.axis_size("obs")
    me = lax.axis_index("obs")
    rows = bw // n_obs_dev
    col_index = jnp.arange(panel_cols, dtype=jnp.int32)

    pieces = owned.reshape(n_obs_dev, rows, panel_cols)
    got = [pieces[me]] + [
        lax.ppermute(pieces[(me + s) % n_obs_dev], "obs", [(i, (i + s) % n_obs_dev) for i in range(n_obs_dev)])
        for s in range(1, n_obs_dev)
    ]
    ordered = jnp.stack(got)
    parts = [ordered[(me - src) % n_obs_dev] for src in range(n_obs_dev)]
    while len(parts) > 1:
        parts = [parts[i] + parts[i + 1] for i in range(0, len(parts), 2)]
    slab = parts[0]
    row_index = my_block * bw + me * rows + jnp.arange(rows, dtype=jnp.int32)
    slab = slab + jnp.where(col_index[None, :] == row_index[:, None], prior_weight[None, :], 0.0)

    inverse = factor_inverse(0.5 * (square[:half] + square[:half].T))
    coupling = jnp.dot(square[half:], inverse.T, precision=HI, preferred_element_type=jnp.float32)
    first_slab = jnp.dot(slab[:, :half], inverse.T, precision=HI, preferred_element_type=jnp.float32)
    update_slab = slab[:, half:] - jnp.dot(
        first_slab, coupling.T, precision=HI, preferred_element_type=jnp.float32
    )
    done = jnp.concatenate([first_slab, update_slab], axis=1)
    spread = [done] + [
        lax.ppermute(done, "obs", [(i, (i + s) % n_obs_dev) for i in range(n_obs_dev)])
        for s in range(1, n_obs_dev)
    ]
    ordered = jnp.stack(spread)
    full = jnp.concatenate([ordered[(me - src) % n_obs_dev] for src in range(n_obs_dev)], axis=0)
    first_rows = full[:, :half]
    update_rows = full[:, half:]
    return (first_rows, update_rows)


def solution(mesh):
    in_specs = (P(("obs", "blk"), None, None), P(("obs", "blk"), None), P(("obs", "blk")), P(), P())
    out_specs = (P("blk", None), P("blk", None))
    return jax.shard_map(local, mesh=mesh, in_specs=in_specs, out_specs=out_specs, check_vma=False)
```

```python
import jax
import jax.numpy as jnp
from jax import lax
from jax.sharding import PartitionSpec as P

CAP = 24
HI = lax.Precision.HIGHEST
FIRST = 8


def dot(a, b):
    return jnp.dot(a, b, precision=HI, preferred_element_type=jnp.float32)


def factor_inverse(mirrored):
    n = mirrored.shape[0] // 2
    eye = jnp.eye(n, dtype=jnp.float32)
    low = jnp.linalg.cholesky(mirrored[:n, :n])
    low_inv = jax.scipy.linalg.solve_triangular(low, eye, lower=True)
    left = dot(mirrored[n:, :n], low_inv.T)
    high = jnp.linalg.cholesky(mirrored[n:, n:] - dot(left, left.T))
    high_inv = jax.scipy.linalg.solve_triangular(high, eye, lower=True)
    corner = -dot(high_inv, dot(left, low_inv))
    return jnp.concatenate(
        [jnp.concatenate([low_inv, jnp.zeros_like(low_inv)], axis=1), jnp.concatenate([corner, high_inv], axis=1)],
        axis=0,
    )


def select_columns(labels, design_tiles, wanted):
    touched = design_tiles.shape[1]
    columns = jnp.zeros(
        (design_tiles.shape[0], wanted.shape[0], design_tiles.shape[2]), jnp.float32
    )
    for entry in range(touched):
        hit = labels[:, entry, None] == wanted[None, :]
        columns = columns + jnp.where(hit[:, :, None], design_tiles[:, entry, None, :], 0.0)
    return columns.reshape(design_tiles.shape[0], wanted.shape[0] * design_tiles.shape[2])


def obs_butterfly(x):
    n = lax.axis_size("obs")
    me = lax.axis_index("obs")
    got = [x] + [lax.ppermute(x, "obs", [(i, (i + s) % n) for i in range(n)]) for s in range(1, n)]
    ordered = jnp.stack(got)
    parts = [ordered[(me - src) % n] for src in range(n)]
    while len(parts) > 1:
        parts = [parts[i] + parts[i + 1] for i in range(0, len(parts), 2)]
    return parts[0]


def ranked(labels, wanted):
    hit = jnp.sum((labels[:, :, None] == wanted[None, None, :]).astype(jnp.int32), axis=1)
    cum = jnp.cumsum(hit, axis=0)
    rank_range = jnp.arange(CAP, dtype=jnp.int32)
    sel = jnp.sum((cum[:, :, None] <= rank_range[None, None, :]).astype(jnp.int32), axis=0)
    valid = rank_range[None, :] < cum[-1][:, None]
    return jnp.minimum(sel, labels.shape[0] - 1), valid


def local(design_tiles, block_ids, obs_weight, block_owner, prior_weight):
    n_obs, touched, bw = design_tiles.shape
    nblk = block_owner.shape[0]
    panel_cols = prior_weight.shape[0]
    half = panel_cols // 2
    panel_blocks = panel_cols // bw
    nb = lax.axis_size("blk")
    my_j = lax.axis_index("blk")
    block_range = jnp.arange(nblk, dtype=jnp.int32)
    dest_range = jnp.arange(nb, dtype=jnp.int32)

    inv_owner = jnp.sum(
        jnp.where(block_owner[None, :] == dest_range[:, None], block_range[None, :], 0), axis=1
    )
    slot_owner = jnp.sum(
        jnp.where(block_ids[:, :, None] == block_range[None, None, :], block_owner[None, None, :], 0),
        axis=2,
    )
    hit = slot_owner[:, :, None] == dest_range[None, None, :]
    touch = jnp.sum(hit.astype(jnp.int32), axis=1)
    cum = jnp.cumsum(touch, axis=0)
    rank_range = jnp.arange(CAP, dtype=jnp.int32)
    obs_sel = jnp.sum((cum[:, :, None] <= rank_range[None, None, :]).astype(jnp.int32), axis=0)
    valid = rank_range[None, :] < cum[-1][:, None]
    obs_sel = jnp.minimum(obs_sel, n_obs - 1)
    owners_sel = slot_owner[obs_sel]
    k_sel = jnp.sum(
        jnp.where(owners_sel == dest_range[:, None, None], jnp.arange(touched, dtype=jnp.int32), 0),
        axis=2,
    )
    flat_tiles = design_tiles.reshape(n_obs * touched, bw)
    tile_rows = flat_tiles[obs_sel * touched + k_sel]

    panel_design = select_columns(
        block_ids, design_tiles, jnp.arange(panel_blocks, dtype=jnp.int32)
    )
    weighted = panel_design * obs_weight[:, None]
    panel_rows = weighted[obs_sel]
    tile_rows = jnp.where(valid[:, :, None], tile_rows, 0.0)
    panel_rows = jnp.where(valid[:, :, None], panel_rows, 0.0)

    gram = jnp.einsum("op,oq->pq", weighted, panel_design[:, :half], precision=HI)
    gram_rows = panel_cols // nb
    got_gram = lax.all_to_all(gram.reshape(nb, gram_rows, half), "blk", 0, 0, tiled=True)
    gram_part = obs_butterfly(jnp.sum(got_gram, axis=0))
    spread = jnp.broadcast_to(gram_part[None], (nb, gram_rows, half))

    panel_range = jnp.arange(panel_blocks, dtype=jnp.int32)
    panel_sel, panel_valid = ranked(block_ids, panel_range)
    panel_tiles = weighted.reshape(n_obs, panel_blocks, bw)[panel_sel, panel_range[:, None]]
    panel_tiles = jnp.where(panel_valid[:, :, None], panel_tiles, 0.0)
    got_gram, panel_tiles = lax.optimization_barrier((got_gram, panel_tiles))
    shared = lax.all_gather(panel_tiles.reshape(-1, bw), "blk", axis=0, tiled=False)

    panel_hit = jnp.sum((block_ids[:, :, None] == panel_range[None, None, :]).astype(jnp.int32), axis=1)
    panel_pos = jnp.where(panel_hit > 0, jnp.cumsum(panel_hit, axis=0) - 1, CAP)
    slot_pos = jnp.where(valid[:, :, None], panel_pos[obs_sel], CAP).astype(jnp.float32)
    index_width = CAP * panel_blocks // gram_rows
    square = lax.all_to_all(spread, "blk", 0, 0, tiled=True).reshape(panel_cols, half)
    payload = jnp.concatenate(
        [tile_rows.reshape(nb, gram_rows, -1), slot_pos.reshape(nb, gram_rows, index_width)], axis=2
    )
    square, payload = lax.optimization_barrier((square, payload))
    got = lax.all_to_all(payload, "blk", 0, 0, tiled=True)
    got_tiles = got[:, :, : CAP * bw // gram_rows].reshape(nb * CAP, bw)
    got_pos = got[:, :, CAP * bw // gram_rows :].reshape(nb, CAP, panel_blocks).astype(jnp.int32)
    diag = jnp.arange(half, dtype=jnp.int32)
    square = square + jnp.where(
        diag[None, :] == jnp.arange(panel_cols, dtype=jnp.int32)[:, None], prior_weight[None, :half], 0.0
    )

    src_panel = shared.reshape(nb, panel_blocks, CAP, bw)
    match = (got_pos[:, :, :, None] == jnp.arange(CAP, dtype=jnp.int32)[None, None, None, :]).astype(jnp.float32)
    slot_panel = jnp.einsum("srpq,spqc->srpc", match, src_panel, precision=HI)
    owned = jnp.einsum(
        "sri,srpc->ipc", got_tiles.reshape(nb, CAP, bw), slot_panel, precision=HI
    ).reshape(bw, panel_cols)
    my_block = jnp.sum(jnp.where(block_owner == my_j, block_range, 0))

    n_obs_dev = lax.axis_size("obs")
    me = lax.axis_index("obs")
    rows = bw // n_obs_dev
    col_index = jnp.arange(panel_cols, dtype=jnp.int32)

    pieces = owned.reshape(n_obs_dev, rows, panel_cols)
    got = [pieces[me]] + [
        lax.ppermute(pieces[(me + s) % n_obs_dev], "obs", [(i, (i + s) % n_obs_dev) for i in range(n_obs_dev)])
        for s in range(1, n_obs_dev)
    ]
    ordered = jnp.stack(got)
    parts = [ordered[(me - src) % n_obs_dev] for src in range(n_obs_dev)]
    while len(parts) > 1:
        parts = [parts[i] + parts[i + 1] for i in range(0, len(parts), 2)]
    slab = parts[0]
    row_index = my_block * bw + me * rows + jnp.arange(rows, dtype=jnp.int32)
    slab = slab + jnp.where(col_index[None, :] == row_index[:, None], prior_weight[None, :], 0.0)

    inverse = factor_inverse(0.5 * (square[:half] + square[:half].T))
    coupling = jnp.dot(square[half:], inverse.T, precision=HI, preferred_element_type=jnp.float32)
    first_slab = jnp.dot(slab[:, :half], inverse.T, precision=HI, preferred_element_type=jnp.float32)
    update_slab = slab[:, half:] - jnp.dot(
        first_slab, coupling.T, precision=HI, preferred_element_type=jnp.float32
    )
    done = jnp.concatenate([first_slab, update_slab], axis=1)
    spread = [done] + [
        lax.ppermute(done, "obs", [(i, (i + s) % n_obs_dev) for i in range(n_obs_dev)])
        for s in range(1, n_obs_dev)
    ]
    ordered = jnp.stack(spread)
    full = jnp.concatenate([ordered[(me - src) % n_obs_dev] for src in range(n_obs_dev)], axis=0)
    first_rows = full[:, :half]
    update_rows = full[:, half:]
    return (first_rows, update_rows)


def solution(mesh):
    in_specs = (P(("obs", "blk"), None, None), P(("obs", "blk"), None), P(("obs", "blk")), P(), P())
    out_specs = (P("blk", None), P("blk", None))
    return jax.shard_map(local, mesh=mesh, in_specs=in_specs, out_specs=out_specs, check_vma=False)
```
